32 devices in a mesh: req: 8 (over y, x, core), head: 4 (over z).
Axes of the slice: x: 2, y: 2, z: 4, core: 2. Of those that a mesh axis runs over, the one named last changes fastest.
Arguments:
- queries: bfloat16 [4096, 8192], P('req', 'head'), may hold values from -150 to 150, as said below
- new_keys: bfloat16 [4096, 1024], P('req', 'head'), may hold values from -6 to 6, as said below
- fresh_values: bfloat16 [4096, 1024], P('req', 'head'), may hold values from -6 to 6
- key_page_pool: bfloat16 [224, 128, 1024], P('req', None, 'head'), may hold values from -6 to 6
- value_page_pool: bfloat16 [224, 128, 1024], P('req', None, 'head'), may hold values from -6 to 6
- page_table: int32 [16, 14], P('req'), may hold values from 0 to 27, as said below
- new_counts: int32 [16], P('req'), may hold values from 1 to 256, 2048 in all
- cached_lens: int32 [16], P('req'), may hold values from 1 to 1536, 8192 in all
- deal_offset: int32 [8], P('req'), may hold values from 0 to 7
- residual: bfloat16 [2112, 8192], P('req', 'head'), may hold values from -1.1953125 to 1.1953125
- out_weight: bfloat16 [8192, 8192], P('head', 'req'), may hold values from -0.09375 to 0.09375
Outputs:
- hidden: bfloat16 [2112, 8192], P('req', 'head')
- keys_out: bfloat16 [224, 128, 1024], P('req', None, 'head')
- values_out: bfloat16 [224, 128, 1024], P('req', None, 'head')
The draws below stay inside these ranges and needn't reach their ends.
Inputs may be any that keep to these rules, and one draw needn't show every extreme that they name: `new_counts`: the counts sum to 2048; the largest is exactly 256. `cached_lens`: the counts sum to 8192; the largest is exactly 1536. `page_table`: the 2 rows of each aligned block of requests hold together each of 0 to 27 once. `queries`: real values. `new_keys`: real values.
All inputs are finite; a program needn't handle non-finite values. No bound on the sum of `new_counts` or of `cached_lens` on one device may be relied on, other than what follows from the above.
Results may differ from the reference program's by a relative error of at most 0.0085.
Values may be sent and summed in bfloat16 or wider, within the bound.
No kernel may reach another device: no remote copies, remote signals or barrier semaphores. Data moves between devices by JAX's collectives and lax.ppermute only.
A program may use at most 128 MiB of HBM per device.

```python
import math
import jax
import jax.numpy as jnp
import numpy as np
from jax import lax

D = 8192
QUERY_HEADS = 64
KEY_VALUE_HEADS = 8
HEAD_SIZE = 128
RPG = 2
NEW_TOKENS_MOST = 256
NEW_MEAN = 128
PAGE_POSITIONS = 128
CTX_PAGES = 12
CTX_MEAN = 512
REQUEST_TOTAL = 16
TABLE_PAGES = 14
BAL = 264
N_REQ = 8
N_HEAD = 4


def shared_draw(key):
    count_of_rows = REQUEST_TOTAL * NEW_TOKENS_MOST
    base_offset = jnp.clip(jax.random.normal(jax.random.fold_in(key, 101), (count_of_rows, KEY_VALUE_HEADS * HEAD_SIZE), jnp.float32), -6.0, 6.0)
    return base_offset


def draw_new_keys(key, part):
    base_offset = shared_draw(key)
    return base_offset.astype(jnp.bfloat16)


def draw_queries(key, part):
    count_of_rows = REQUEST_TOTAL * NEW_TOKENS_MOST
    drawn = jnp.clip(jax.random.normal(jax.random.fold_in(key, 104), (count_of_rows, QUERY_HEADS * HEAD_SIZE), jnp.float32), -6.0, 6.0)
    return drawn.astype(jnp.bfloat16)


def draw_page_table(key, part):
    pool_size = RPG * TABLE_PAGES
    block_ids = jnp.arange(REQUEST_TOTAL // RPG)
    perms = jax.vmap(lambda block_id: jax.random.permutation(jax.random.fold_in(key, block_id), pool_size))(block_ids)
    return perms.reshape(REQUEST_TOTAL, TABLE_PAGES).astype(jnp.int32)


def place_ends(values, key, smallest, largest):
    longest = values.shape.index(max(values.shape))
    spots = []
    for shift in (0, 1):
        where = [jax.random.randint(jax.random.fold_in(key, axis), (), 0, length) for axis, length in enumerate(values.shape)]
        where[longest] = (where[longest] + shift) % values.shape[longest]
        spots.append(tuple(where))
    return values.at[spots[0]].set(smallest).at[spots[1]].set(largest)


def with_spikes(entries, key, source, target, blocks, factor):
    owner, partner = [(jnp.arange(entries.shape[dim]) // (entries.shape[dim] // blocks)).reshape([-1 if axis == dim else 1 for axis in range(entries.ndim)]) for dim in (source, target)]
    chosen = jax.random.permutation(key, blocks)[partner]
    strong = (owner == chosen) | (owner == (partner + blocks // 2) % blocks)
    return jnp.where(strong, factor * entries, entries)


def block_levels(key, shape, split, least, largest):
    level, own = 1.0, jax.random.fold_in(key, 6)
    for position, shards_of in split:
        heights = jnp.exp(jax.random.uniform(jax.random.fold_in(own, position), (shards_of,), jnp.float32, least / len(split), largest / len(split)))
        level = level * jnp.repeat(heights, shape[position] // shards_of).reshape([-1 if axis == position else 1 for axis in range(len(shape))])
    return level


def length_profile(number_of, total, reach, skew):
    loads = [(1 << 20) // math.isqrt(standing ** skew) + 1 for standing in range(2, number_of + 1)]
    rest, holding = total - reach - (number_of - 1), [1] * (number_of - 1)
    while rest > 0:
        free = [i for i in range(number_of - 1) if holding[i] < reach]
        pool, budget = sum([loads[i] for i in free]), rest
        for i in free:
            more = min(reach - holding[i], max(1, budget * loads[i] // pool), rest)
            holding[i] = holding[i] + more
            rest = rest - more
    return np.array([reach] + holding)


def uneven(stream_key, count, total, bound, skew):
    if count == 2:
        one = jax.random.randint(stream_key, (), max(1, total - bound), min(bound, total - 1) + 1)
        return jnp.stack([one, total - one])
    sizes = jnp.asarray(length_profile(count, total, bound, skew), jnp.int32)
    pairs = (count - 1) // 2
    giver, sink = sizes[1:1 + 2 * pairs:2], sizes[2:2 + 2 * pairs:2]
    room = jnp.minimum(giver - 1, bound - sink)
    passed = jax.random.randint(jax.random.fold_in(stream_key, 1), (pairs,), 0, 1 << 20) % (room + 1)
    sizes = sizes.at[1:1 + 2 * pairs:2].set(giver - passed).at[2:2 + 2 * pairs:2].set(sink + passed)
    return sizes[jax.random.permutation(jax.random.fold_in(stream_key, 2), count)]


def scatter_about(key, shape, width, bound, split=(), held_as=jnp.bfloat16):
    values = width * jax.random.normal(key, shape, jnp.float32)
    if split:
        values = values * block_levels(key, shape, split, -0.22, 0.18)
    return jnp.clip(values, -bound, bound).astype(held_as)


def noise_with(key, shape, width, reach, split, heavy, kind=jnp.bfloat16):
    result = width * jax.random.normal(key, shape, jnp.float32)
    if split:
        result = result * block_levels(key, shape, split, -0.22, 0.18)
    return jnp.clip(with_spikes(result, jax.random.fold_in(key, 3), *heavy), -reach, reach).astype(kind)


def setup_inputs(seed: int = 0) -> dict:
    splits = jax.random.split(jax.random.key(seed), 12)
    return {
        "queries": draw_queries(jax.random.fold_in(splits[11], 71), 0),
        "new_keys": draw_new_keys(jax.random.fold_in(splits[11], 71), 0),
        "fresh_values": scatter_about(splits[2], (REQUEST_TOTAL * NEW_TOKENS_MOST, KEY_VALUE_HEADS * HEAD_SIZE), 1.0, 6.0, ((0, 8), (1, 4))),
        "key_page_pool": scatter_about(splits[3], (REQUEST_TOTAL * TABLE_PAGES, PAGE_POSITIONS, KEY_VALUE_HEADS * HEAD_SIZE), 1.0, 6.0, ((0, 8), (2, 4))),
        "value_page_pool": scatter_about(splits[4], (REQUEST_TOTAL * TABLE_PAGES, PAGE_POSITIONS, KEY_VALUE_HEADS * HEAD_SIZE), 1.0, 6.0, ((0, 8), (2, 4))),
        "page_table": draw_page_table(jax.random.fold_in(splits[11], 71), 0),
        "new_counts": uneven(splits[6], REQUEST_TOTAL, REQUEST_TOTAL * NEW_MEAN, NEW_TOKENS_MOST, 2).astype(jnp.int32),
        "cached_lens": uneven(splits[7], REQUEST_TOTAL, REQUEST_TOTAL * CTX_MEAN, CTX_PAGES * PAGE_POSITIONS, 2).astype(jnp.int32),
        "deal_offset": place_ends(jax.random.randint(splits[8], (N_REQ,), 0, N_REQ), jax.random.fold_in(splits[8], 1), 0, N_REQ - 1).astype(jnp.int32),
        "residual": scatter_about(splits[9], (N_REQ * BAL, D), 0.2, 1.1953125, ((0, 8), (1, 4))),
        "out_weight": noise_with(splits[10], (QUERY_HEADS * HEAD_SIZE, D), (QUERY_HEADS * HEAD_SIZE) ** -0.5, 0.09375, ((0, 4), (1, 8)), (0, 1, 8, 2.0)),
    }


NEGATIVE = -1e+30

def reference(queries, new_keys, fresh_values, key_page_pool, value_page_pool, page_table, new_counts, cached_lens, deal_offset, residual, out_weight):
    channel_count = KEY_VALUE_HEADS * HEAD_SIZE
    group_fanout = QUERY_HEADS // KEY_VALUE_HEADS
    pool_size = RPG * TABLE_PAGES
    owner = jnp.arange(REQUEST_TOTAL, dtype=jnp.int32) // RPG
    pool_page_index = (page_table + (owner * pool_size)[:, None]).astype(jnp.int32)
    new_slot = jnp.arange(NEW_TOKENS_MOST, dtype=jnp.int32)
    positions = (cached_lens[:, None] + new_slot[None, :]).astype(jnp.int32)
    page_of = jnp.take_along_axis(pool_page_index, positions // PAGE_POSITIONS, axis=1)
    outside = REQUEST_TOTAL * TABLE_PAGES * PAGE_POSITIONS
    is_live = new_slot[None, :] < new_counts[:, None]
    target = jnp.where(is_live, page_of * PAGE_POSITIONS + positions % PAGE_POSITIONS, outside).reshape(-1)
    flat_keys = key_page_pool.reshape(-1, channel_count).at[target].set(new_keys, mode='drop')
    flat_values = value_page_pool.reshape(-1, channel_count).at[target].set(fresh_values, mode='drop')
    gathered_keys = flat_keys.reshape(-1, PAGE_POSITIONS, channel_count)
    gathered_values = flat_values.reshape(-1, PAGE_POSITIONS, channel_count)
    scale_factor = 1.0 / math.sqrt(HEAD_SIZE)
    spots_all = jnp.arange(TABLE_PAGES * PAGE_POSITIONS, dtype=jnp.int32)

    def attend(request_index):
        prior_keys = gathered_keys[pool_page_index[request_index]].reshape(TABLE_PAGES * PAGE_POSITIONS, KEY_VALUE_HEADS, HEAD_SIZE).astype(jnp.float32)
        prior_values = gathered_values[pool_page_index[request_index]].reshape(TABLE_PAGES * PAGE_POSITIONS, KEY_VALUE_HEADS, HEAD_SIZE).astype(jnp.float32)
        query_matrix = lax.dynamic_slice_in_dim(queries, request_index * NEW_TOKENS_MOST, NEW_TOKENS_MOST, 0)
        query_matrix = query_matrix.reshape(NEW_TOKENS_MOST, KEY_VALUE_HEADS, group_fanout, HEAD_SIZE).astype(jnp.float32)
        scores = jnp.einsum('tkgd,skd->kgts', query_matrix, prior_keys) * scale_factor
        allowed = spots_all[None, :] <= positions[request_index][:, None]
        scores = jnp.where(allowed, scores, NEGATIVE)
        highest = lax.optimization_barrier(jnp.max(scores, axis=3, keepdims=True))
        expo_terms = jnp.where(allowed, jnp.exp(scores - highest), 0.0)
        weights = (expo_terms / lax.optimization_barrier(jnp.sum(expo_terms, axis=3, keepdims=True))).astype(jnp.bfloat16)
        mixed = jnp.einsum('kgts,skd->tkgd', weights.astype(jnp.float32), prior_values)
        return mixed.astype(jnp.bfloat16).reshape(NEW_TOKENS_MOST, QUERY_HEADS * HEAD_SIZE)
    attended = lax.map(attend, jnp.arange(REQUEST_TOTAL, dtype=jnp.int32)).reshape(REQUEST_TOTAL * NEW_TOKENS_MOST, QUERY_HEADS * HEAD_SIZE)
    share = QUERY_HEADS * HEAD_SIZE // N_HEAD
    total_sum = jnp.zeros((REQUEST_TOTAL * NEW_TOKENS_MOST, D), jnp.float32)
    for member in range(N_HEAD):
        partial_sum = jnp.dot(attended[:, member * share:(member + 1) * share], out_weight[member * share:(member + 1) * share], preferred_element_type=jnp.float32)
        rounded = lax.optimization_barrier(partial_sum.astype(jnp.bfloat16))
        total_sum = total_sum + rounded.astype(jnp.float32)
    projected = total_sum.astype(jnp.bfloat16)
    counts_grid = new_counts.reshape(N_REQ, RPG)
    totals = lax.optimization_barrier(jnp.sum(counts_grid, axis=1)).astype(jnp.int32)
    rank_ids = jnp.arange(N_REQ, dtype=jnp.int32)
    lead_in = jnp.remainder(rank_ids[None, :] - deal_offset[:, None], N_REQ).astype(jnp.int32)
    shares = jnp.maximum((totals[:, None] - lead_in + N_REQ - 1) // N_REQ, 0).astype(jnp.int32)
    starts = (jnp.cumsum(shares, axis=0) - shares).astype(jnp.int32)
    within = (jnp.cumsum(counts_grid, axis=1) - counts_grid).reshape(-1).astype(jnp.int32)
    ordinal = (within[:, None] + new_slot[None, :]).astype(jnp.int32)
    dest_rank = jnp.remainder(ordinal + deal_offset[owner][:, None], N_REQ).astype(jnp.int32)
    owner_grid = jnp.broadcast_to(owner[:, None], dest_rank.shape)
    dest_row = dest_rank * BAL + starts[owner_grid, dest_rank] + ordinal // N_REQ
    dest_row = jnp.where(is_live, dest_row, N_REQ * BAL).reshape(-1)
    placed = jnp.zeros((N_REQ * BAL, D), jnp.bfloat16).at[dest_row].set(projected, mode='drop')
    hidden = (residual.astype(jnp.float32) + placed.astype(jnp.float32)).astype(jnp.bfloat16)
    return (hidden, flat_keys.reshape(key_page_pool.shape), flat_values.reshape(value_page_pool.shape))
```

```python
import math

import jax
import jax.numpy as jnp
from jax import lax
from jax.sharding import PartitionSpec as P

HEAD_SIZE = 128


NEGATIVE = -1e30


def head_attention(query_matrix, prior_keys, prior_values, visible, scale_factor):
    scores = (
        jnp.einsum("tkd,skd->kts", query_matrix, prior_keys, preferred_element_type=jnp.float32)
        * scale_factor
    )
    spots_all = jnp.arange(prior_keys.shape[0], dtype=jnp.int32)
    allowed = spots_all[None, None, :] <= visible[None, :, None]
    scores = jnp.where(allowed, scores, NEGATIVE)
    highest = jnp.max(scores, axis=2, keepdims=True)
    expo_terms = jnp.where(allowed, jnp.exp(scores - highest), 0.0)
    weights = (expo_terms / jnp.sum(expo_terms, axis=2, keepdims=True)).astype(jnp.bfloat16)
    mixed = jnp.einsum("kts,skd->tkd", weights, prior_values, preferred_element_type=jnp.float32)
    return mixed.astype(jnp.bfloat16)


def deal(row_block, new_counts, lead_in, shares, starts, totals, balanced):
    groups = lax.axis_size("req")
    my_rank = lax.axis_index("req")
    per_group = new_counts.shape[0]
    new_limit = row_block.shape[0] // per_group
    pair_slots = row_block.shape[0] // groups
    columns = row_block.shape[1]
    own_lead = lax.dynamic_index_in_dim(lead_in, my_rank, 0, keepdims=False)
    ordinal = jnp.arange(pair_slots, dtype=jnp.int32)[None, :] * groups + own_lead[:, None]
    ends_at = jnp.cumsum(new_counts)
    request_index = jnp.sum(
        (ordinal[:, :, None] >= ends_at[None, None, :]).astype(jnp.int32), axis=2
    )
    request_index = jnp.minimum(request_index, per_group - 1)
    before = ends_at - new_counts
    source = request_index * new_limit + ordinal - jnp.take(before, request_index)
    own_total = lax.dynamic_index_in_dim(totals, my_rank, 0, keepdims=False)
    is_live = ordinal < own_total
    source = jnp.where(is_live, source, 0)
    picked = jnp.take(row_block, source.reshape(-1), axis=0).reshape(groups, pair_slots, columns)
    outgoing = jnp.where(is_live[:, :, None], picked, jnp.zeros((), row_block.dtype))
    arrived = lax.all_to_all(outgoing, "req", split_axis=0, concat_axis=0, tiled=True)
    own_shares = lax.dynamic_index_in_dim(shares, my_rank, 1, keepdims=False)
    own_starts = lax.dynamic_index_in_dim(starts, my_rank, 1, keepdims=False)
    within = jnp.arange(pair_slots, dtype=jnp.int32)[None, :]
    landing = jnp.where(within < own_shares[:, None], own_starts[:, None] + within, balanced)
    blank_rows = jnp.zeros((balanced, columns), row_block.dtype)
    return blank_rows.at[landing.reshape(-1)].set(arrived.reshape(-1, columns), mode="drop")


def project(row_block, out_weight):
    return jnp.dot(
        row_block,
        lax.all_gather(out_weight, "req", axis=1, tiled=True),
        preferred_element_type=jnp.float32,
    )


def head_total(partial_sum):
    return lax.psum_scatter(
        partial_sum.astype(jnp.bfloat16), "head", scatter_dimension=1, tiled=True
    ).astype(jnp.float32)


def local(
    queries,
    new_keys,
    fresh_values,
    key_page_pool,
    value_page_pool,
    page_table,
    new_counts,
    cached_lens,
    deal_offset,
    residual,
    out_weight,
):
    groups = lax.axis_size("req")
    per_group = new_counts.shape[0]
    page_count = page_table.shape[1]
    page_rows = key_page_pool.shape[1]
    channel_count = key_page_pool.shape[2]
    kv_local = channel_count // HEAD_SIZE
    slot_count = queries.shape[0]
    new_limit = slot_count // per_group
    q_width = queries.shape[1]
    group_fanout = q_width // channel_count
    balanced = residual.shape[0]
    new_slot = jnp.arange(new_limit, dtype=jnp.int32)
    positions = cached_lens[:, None] + new_slot[None, :]
    page_of = jnp.take_along_axis(page_table, positions // page_rows, axis=1)
    outside = key_page_pool.shape[0] * page_rows
    target = jnp.where(
        new_slot[None, :] < new_counts[:, None],
        page_of * page_rows + positions % page_rows,
        outside,
    ).reshape(-1)
    flat_keys = key_page_pool.reshape(-1, channel_count).at[target].set(new_keys, mode="drop")
    flat_values = (
        value_page_pool.reshape(-1, channel_count).at[target].set(fresh_values, mode="drop")
    )
    gathered_keys = flat_keys.reshape(key_page_pool.shape)
    gathered_values = flat_values.reshape(value_page_pool.shape)
    scale_factor = 1.0 / math.sqrt(HEAD_SIZE)
    pieces = []
    for member in range(per_group):
        prior_keys = gathered_keys[page_table[member]].reshape(
            page_count * page_rows, kv_local, HEAD_SIZE
        )
        prior_values = gathered_values[page_table[member]].reshape(
            page_count * page_rows, kv_local, HEAD_SIZE
        )
        query_matrix = queries[member * new_limit : (member + 1) * new_limit].reshape(
            new_limit, kv_local, group_fanout, HEAD_SIZE
        )
        query_matrix = jnp.moveaxis(query_matrix, 2, 0)
        visible = positions[member]
        mixed = lax.map(
            lambda single: head_attention(single, prior_keys, prior_values, visible, scale_factor),
            query_matrix,
        )
        pieces.append(jnp.moveaxis(mixed, 0, 2).reshape(new_limit, q_width))
    attended = jnp.concatenate(pieces, axis=0)
    load_counts, offsets_all = (
        lax.all_gather(new_counts, "req", axis=0, tiled=True),
        lax.all_gather(deal_offset, "req", axis=0, tiled=True),
    )
    totals = jnp.sum(load_counts.reshape(groups, per_group), axis=1)
    rank_ids = jnp.arange(groups, dtype=jnp.int32)
    lead_in = jnp.remainder(rank_ids[None, :] - offsets_all[:, None], groups)
    shares = jnp.maximum((totals[:, None] - lead_in + groups - 1) // groups, 0)
    starts = jnp.cumsum(shares, axis=0) - shares
    placed = deal(attended, new_counts, lead_in, shares, starts, totals, balanced)
    summed = head_total(project(placed, out_weight)).astype(jnp.bfloat16)
    hidden = (residual.astype(jnp.float32) + summed.astype(jnp.float32)).astype(jnp.bfloat16)
    return (hidden, gathered_keys, gathered_values)


def solution(mesh):
    placed = (
        P("req", "head"),
        P("req", "head"),
        P("req", "head"),
        P("req", None, "head"),
        P("req", None, "head"),
        P("req", None),
        P("req"),
        P("req"),
        P("req"),
        P("req", "head"),
        P("head", "req"),
    )
    return jax.shard_map(
        local,
        mesh=mesh,
        in_specs=placed,
        out_specs=(P("req", "head"), P("req", None, "head"), P("req", None, "head")),
        check_vma=False,
    )
```

```python
import math

import jax
import jax.numpy as jnp
from jax import lax
from jax.sharding import PartitionSpec as P
from jax.experimental import pallas as pl
from jax.experimental.pallas import tpu as pltpu

HEAD_SIZE = 128


NEGATIVE = -1e30


def attention_kernel(cached_ref, q_ref, k_ref, v_ref, o_ref, *, fanout, scale_factor):
    member = pl.program_id(0)
    rows = q_ref.shape[0]
    spots = k_ref.shape[0]
    row_ids = lax.broadcasted_iota(jnp.int32, (rows, spots), 0)
    col_ids = lax.broadcasted_iota(jnp.int32, (rows, spots), 1)
    allowed = col_ids <= row_ids + cached_ref[member]
    keys = k_ref[...]
    values = v_ref[...]
    for head in range(fanout):
        lanes = slice(head * HEAD_SIZE, (head + 1) * HEAD_SIZE)
        scores = (
            lax.dot_general(
                q_ref[:, lanes], keys, (((1,), (1,)), ((), ())),
                preferred_element_type=jnp.float32,
            )
            * scale_factor
        )
        scores = jnp.where(allowed, scores, NEGATIVE)
        highest = jnp.max(scores, axis=1, keepdims=True)
        expo_terms = jnp.exp(scores - highest)
        weights = (expo_terms / jnp.sum(expo_terms, axis=1, keepdims=True)).astype(jnp.bfloat16)
        mixed = jnp.dot(weights, values, preferred_element_type=jnp.float32)
        o_ref[:, lanes] = mixed.astype(o_ref.dtype)


def paged_attention(queries, prior_keys, prior_values, cached_lens, fanout, scale_factor):
    per_group, spots, channel_count = prior_keys.shape
    kv_local = channel_count // HEAD_SIZE
    new_limit = queries.shape[0] // per_group
    width = fanout * HEAD_SIZE
    kernel = lambda *refs: attention_kernel(*refs, fanout=fanout, scale_factor=scale_factor)
    return pl.pallas_call(
        kernel,
        grid_spec=pltpu.PrefetchScalarGridSpec(
            num_scalar_prefetch=1,
            grid=(per_group, kv_local),
            in_specs=[
                pl.BlockSpec((new_limit, width), lambda m, g, c: (m, g)),
                pl.BlockSpec((None, spots, HEAD_SIZE), lambda m, g, c: (m, 0, g)),
                pl.BlockSpec((None, spots, HEAD_SIZE), lambda m, g, c: (m, 0, g)),
            ],
            out_specs=pl.BlockSpec((new_limit, width), lambda m, g, c: (m, g)),
        ),
        out_shape=jax.ShapeDtypeStruct(queries.shape, jnp.bfloat16),
        compiler_params=pltpu.CompilerParams(
            dimension_semantics=("arbitrary", "arbitrary"),
        ),
    )(cached_lens, queries, prior_keys, prior_values)


def deal(row_block, new_counts, lead_in, shares, starts, totals, balanced):
    groups = lax.axis_size("req")
    my_rank = lax.axis_index("req")
    per_group = new_counts.shape[0]
    new_limit = row_block.shape[0] // per_group
    pair_slots = row_block.shape[0] // groups
    columns = row_block.shape[1]
    own_lead = lax.dynamic_index_in_dim(lead_in, my_rank, 0, keepdims=False)
    ordinal = jnp.arange(pair_slots, dtype=jnp.int32)[None, :] * groups + own_lead[:, None]
    ends_at = jnp.cumsum(new_counts)
    request_index = jnp.sum(
        (ordinal[:, :, None] >= ends_at[None, None, :]).astype(jnp.int32), axis=2
    )
    request_index = jnp.minimum(request_index, per_group - 1)
    before = ends_at - new_counts
    source = request_index * new_limit + ordinal - jnp.take(before, request_index)
    own_total = lax.dynamic_index_in_dim(totals, my_rank, 0, keepdims=False)
    is_live = ordinal < own_total
    source = jnp.where(is_live, source, 0)
    picked = jnp.take(row_block, source.reshape(-1), axis=0).reshape(groups, pair_slots, columns)
    outgoing = jnp.where(is_live[:, :, None], picked, jnp.zeros((), row_block.dtype))
    arrived = lax.all_to_all(outgoing, "req", split_axis=0, concat_axis=0, tiled=True)
    own_shares = lax.dynamic_index_in_dim(shares, my_rank, 1, keepdims=False)
    own_starts = lax.dynamic_index_in_dim(starts, my_rank, 1, keepdims=False)
    within = jnp.arange(pair_slots, dtype=jnp.int32)[None, :]
    landing = jnp.where(within < own_shares[:, None], own_starts[:, None] + within, balanced)
    blank_rows = jnp.zeros((balanced, columns), row_block.dtype)
    return blank_rows.at[landing.reshape(-1)].set(arrived.reshape(-1, columns), mode="drop")


def project(row_block, out_weight):
    return jnp.dot(
        row_block,
        lax.all_gather(out_weight, "req", axis=1, tiled=True),
        preferred_element_type=jnp.float32,
    )


def head_total(partial_sum):
    return lax.psum_scatter(
        partial_sum.astype(jnp.bfloat16), "head", scatter_dimension=1, tiled=True
    ).astype(jnp.float32)


def local(
    queries,
    new_keys,
    fresh_values,
    key_page_pool,
    value_page_pool,
    page_table,
    new_counts,
    cached_lens,
    deal_offset,
    residual,
    out_weight,
):
    groups = lax.axis_size("req")
    per_group = new_counts.shape[0]
    page_count = page_table.shape[1]
    page_rows = key_page_pool.shape[1]
    channel_count = key_page_pool.shape[2]
    kv_local = channel_count // HEAD_SIZE
    slot_count = queries.shape[0]
    new_limit = slot_count // per_group
    q_width = queries.shape[1]
    group_fanout = q_width // channel_count
    balanced = residual.shape[0]
    new_slot = jnp.arange(new_limit, dtype=jnp.int32)
    positions = cached_lens[:, None] + new_slot[None, :]
    page_of = jnp.take_along_axis(page_table, positions // page_rows, axis=1)
    outside = key_page_pool.shape[0] * page_rows
    target = jnp.where(
        new_slot[None, :] < new_counts[:, None],
        page_of * page_rows + positions % page_rows,
        outside,
    ).reshape(-1)
    flat_keys = key_page_pool.reshape(-1, channel_count).at[target].set(new_keys, mode="drop")
    flat_values = (
        value_page_pool.reshape(-1, channel_count).at[target].set(fresh_values, mode="drop")
    )
    gathered_keys = flat_keys.reshape(key_page_pool.shape)
    gathered_values = flat_values.reshape(value_page_pool.shape)
    scale_factor = 1.0 / math.sqrt(HEAD_SIZE)
    table = page_table
    prior_keys = gathered_keys[table].reshape(per_group, page_count * page_rows, channel_count)
    prior_values = gathered_values[table].reshape(per_group, page_count * page_rows, channel_count)
    attended = paged_attention(
        queries, prior_keys, prior_values, cached_lens, group_fanout, scale_factor
    )
    load_counts, offsets_all = (
        lax.all_gather(new_counts, "req", axis=0, tiled=True),
        lax.all_gather(deal_offset, "req", axis=0, tiled=True),
    )
    totals = jnp.sum(load_counts.reshape(groups, per_group), axis=1)
    rank_ids = jnp.arange(groups, dtype=jnp.int32)
    lead_in = jnp.remainder(rank_ids[None, :] - offsets_all[:, None], groups)
    shares = jnp.maximum((totals[:, None] - lead_in + groups - 1) // groups, 0)
    starts = jnp.cumsum(shares, axis=0) - shares
    placed = deal(attended, new_counts, lead_in, shares, starts, totals, balanced)
    summed = head_total(project(placed, out_weight)).astype(jnp.bfloat16)
    hidden = (residual.astype(jnp.float32) + summed.astype(jnp.float32)).astype(jnp.bfloat16)
    return (hidden, gathered_keys, gathered_values)


def solution(mesh):
    placed = (
        P("req", "head"),
        P("req", "head"),
        P("req", "head"),
        P("req", None, "head"),
        P("req", None, "head"),
        P("req", None),
        P("req"),
        P("req"),
        P("req"),
        P("req", "head"),
        P("head", "req"),
    )
    return jax.shard_map(
        local,
        mesh=mesh,
        in_specs=placed,
        out_specs=(P("req", "head"), P("req", None, "head"), P("req", None, "head")),
        check_vma=False,
    )
```

```python
import math

import jax
import jax.numpy as jnp
from jax import lax
from jax.sharding import PartitionSpec as P
from jax.experimental import pallas as pl
from jax.experimental.pallas import tpu as pltpu

HEAD_SIZE = 128


NEGATIVE = -1e30


def attention_kernel(cached_ref, q_ref, k_ref, v_ref, o_ref, *, fanout, scale_factor):
    member = pl.program_id(0)
    rows = q_ref.shape[0]
    spots = k_ref.shape[0]
    row_ids = lax.broadcasted_iota(jnp.int32, (rows, spots), 0)
    col_ids = lax.broadcasted_iota(jnp.int32, (rows, spots), 1)
    allowed = col_ids <= row_ids + cached_ref[member]
    keys = k_ref[...]
    values = v_ref[...]
    for head in range(fanout):
        lanes = slice(head * HEAD_SIZE, (head + 1) * HEAD_SIZE)
        scores = (
            lax.dot_general(
                q_ref[:, lanes], keys, (((1,), (1,)), ((), ())),
                preferred_element_type=jnp.float32,
            )
            * scale_factor
        )
        scores = jnp.where(allowed, scores, NEGATIVE)
        highest = jnp.max(scores, axis=1, keepdims=True)
        expo_terms = jnp.exp(scores - highest)
        weights = (expo_terms / jnp.sum(expo_terms, axis=1, keepdims=True)).astype(jnp.bfloat16)
        mixed = jnp.dot(weights, values, preferred_element_type=jnp.float32)
        o_ref[:, lanes] = mixed.astype(o_ref.dtype)


def paged_attention(queries, prior_keys, prior_values, cached_lens, fanout, scale_factor):
    per_group, spots, channel_count = prior_keys.shape
    kv_local = channel_count // HEAD_SIZE
    new_limit = queries.shape[0] // per_group
    width = fanout * HEAD_SIZE
    kernel = lambda *refs: attention_kernel(*refs, fanout=fanout, scale_factor=scale_factor)
    return pl.pallas_call(
        kernel,
        grid_spec=pltpu.PrefetchScalarGridSpec(
            num_scalar_prefetch=1,
            grid=(per_group, kv_local),
            in_specs=[
                pl.BlockSpec((new_limit, width), lambda m, g, c: (m, g)),
                pl.BlockSpec((None, spots, HEAD_SIZE), lambda m, g, c: (m, 0, g)),
                pl.BlockSpec((None, spots, HEAD_SIZE), lambda m, g, c: (m, 0, g)),
            ],
            out_specs=pl.BlockSpec((new_limit, width), lambda m, g, c: (m, g)),
        ),
        out_shape=jax.ShapeDtypeStruct(queries.shape, jnp.bfloat16),
        compiler_params=pltpu.CompilerParams(
            dimension_semantics=("arbitrary", "arbitrary"),
        ),
    )(cached_lens, queries, prior_keys, prior_values)


def deal(row_block, new_counts, lead_in, shares, starts, totals, balanced):
    groups = lax.axis_size("req")
    my_rank = lax.axis_index("req")
    per_group = new_counts.shape[0]
    new_limit = row_block.shape[0] // per_group
    pair_slots = row_block.shape[0] // groups
    columns = row_block.shape[1]
    own_lead = lax.dynamic_index_in_dim(lead_in, my_rank, 0, keepdims=False)
    ordinal = jnp.arange(pair_slots, dtype=jnp.int32)[None, :] * groups + own_lead[:, None]
    ends_at = jnp.cumsum(new_counts)
    request_index = jnp.sum(
        (ordinal[:, :, None] >= ends_at[None, None, :]).astype(jnp.int32), axis=2
    )
    request_index = jnp.minimum(request_index, per_group - 1)
    before = ends_at - new_counts
    source = request_index * new_limit + ordinal - jnp.take(before, request_index)
    own_total = lax.dynamic_index_in_dim(totals, my_rank, 0, keepdims=False)
    is_live = ordinal < own_total
    source = jnp.where(is_live, source, 0)
    picked = jnp.take(row_block, source.reshape(-1), axis=0).reshape(groups, pair_slots, columns)
    outgoing = jnp.where(is_live[:, :, None], picked, jnp.zeros((), row_block.dtype))
    arrived = lax.all_to_all(outgoing, "req", split_axis=0, concat_axis=0, tiled=True)
    own_shares = lax.dynamic_index_in_dim(shares, my_rank, 1, keepdims=False)
    own_starts = lax.dynamic_index_in_dim(starts, my_rank, 1, keepdims=False)
    within = jnp.arange(pair_slots, dtype=jnp.int32)[None, :]
    landing = jnp.where(within < own_shares[:, None], own_starts[:, None] + within, balanced)
    blank_rows = jnp.zeros((balanced, columns), row_block.dtype)
    return blank_rows.at[landing.reshape(-1)].set(arrived.reshape(-1, columns), mode="drop")


def paired_rows(block, partner, first):
    return jnp.where(first, jnp.concatenate([block, partner]), jnp.concatenate([partner, block]))


def project_and_sum(row_block, out_weight):
    groups = lax.axis_size("req")
    head_groups = lax.axis_size("head")
    my_rank = lax.axis_index("req")
    is_first = my_rank % 2 == 0
    pair_perm = [(i, i ^ 1) for i in range(groups)]
    half = groups // 2
    weight_blocks = [out_weight]
    for step in range(1, half):
        weight_blocks.append(
            lax.ppermute(out_weight, "req", [(i, i ^ (2 * step)) for i in range(groups)])
        )
    order = jnp.arange(half, dtype=jnp.int32) ^ (my_rank // 2)
    weight_sorted = jnp.take(jnp.stack(weight_blocks), order, axis=0)
    inner, block_cols = out_weight.shape
    weight_sorted = jnp.moveaxis(weight_sorted, 0, 1).reshape(inner, half * block_cols)
    rows = row_block.shape[0]
    both_rows = paired_rows(row_block, lax.ppermute(row_block, "req", pair_perm), is_first)
    partial_sum = jnp.dot(both_rows, weight_sorted, preferred_element_type=jnp.float32)
    per_chunk = half // head_groups
    partial_sum = partial_sum.astype(jnp.bfloat16).reshape(2 * rows, head_groups, per_chunk * block_cols)
    reduced = lax.psum_scatter(
        jnp.moveaxis(partial_sum, 1, 0), "head", scatter_dimension=0, tiled=True
    )[0]
    own_rows = jnp.where(is_first, reduced[:rows], reduced[rows:])
    other_rows = jnp.where(is_first, reduced[rows:], reduced[:rows])
    arrived = lax.ppermute(other_rows, "req", pair_perm)
    mine = own_rows.reshape(rows, per_chunk, block_cols)
    theirs = arrived.reshape(rows, per_chunk, block_cols)
    even = jnp.where(is_first, mine, theirs)
    odd = jnp.where(is_first, theirs, mine)
    return jnp.stack([even, odd], axis=2).reshape(rows, 2 * per_chunk * block_cols)


def local(
    queries,
    new_keys,
    fresh_values,
    key_page_pool,
    value_page_pool,
    page_table,
    new_counts,
    cached_lens,
    deal_offset,
    residual,
    out_weight,
):
    groups = lax.axis_size("req")
    per_group = new_counts.shape[0]
    page_count = page_table.shape[1]
    page_rows = key_page_pool.shape[1]
    channel_count = key_page_pool.shape[2]
    kv_local = channel_count // HEAD_SIZE
    slot_count = queries.shape[0]
    new_limit = slot_count // per_group
    q_width = queries.shape[1]
    group_fanout = q_width // channel_count
    balanced = residual.shape[0]
    new_slot = jnp.arange(new_limit, dtype=jnp.int32)
    positions = cached_lens[:, None] + new_slot[None, :]
    page_of = jnp.take_along_axis(page_table, positions // page_rows, axis=1)
    outside = key_page_pool.shape[0] * page_rows
    target = jnp.where(
        new_slot[None, :] < new_counts[:, None],
        page_of * page_rows + positions % page_rows,
        outside,
    ).reshape(-1)
    flat_keys = key_page_pool.reshape(-1, channel_count).at[target].set(new_keys, mode="drop")
    flat_values = (
        value_page_pool.reshape(-1, channel_count).at[target].set(fresh_values, mode="drop")
    )
    gathered_keys = flat_keys.reshape(key_page_pool.shape)
    gathered_values = flat_values.reshape(value_page_pool.shape)
    scale_factor = 1.0 / math.sqrt(HEAD_SIZE)
    table = page_table
    prior_keys = gathered_keys[table].reshape(per_group, page_count * page_rows, channel_count)
    prior_values = gathered_values[table].reshape(per_group, page_count * page_rows, channel_count)
    attended = paged_attention(
        queries, prior_keys, prior_values, cached_lens, group_fanout, scale_factor
    )
    load_counts, offsets_all = (
        lax.all_gather(new_counts, "req", axis=0, tiled=True),
        lax.all_gather(deal_offset, "req", axis=0, tiled=True),
    )
    totals = jnp.sum(load_counts.reshape(groups, per_group), axis=1)
    rank_ids = jnp.arange(groups, dtype=jnp.int32)
    lead_in = jnp.remainder(rank_ids[None, :] - offsets_all[:, None], groups)
    shares = jnp.maximum((totals[:, None] - lead_in + groups - 1) // groups, 0)
    starts = jnp.cumsum(shares, axis=0) - shares
    placed = deal(attended, new_counts, lead_in, shares, starts, totals, balanced)
    summed = project_and_sum(placed, out_weight)
    hidden = (residual.astype(jnp.float32) + summed.astype(jnp.float32)).astype(jnp.bfloat16)
    return (hidden, gathered_keys, gathered_values)


def solution(mesh):
    placed = (
        P("req", "head"),
        P("req", "head"),
        P("req", "head"),
        P("req", None, "head"),
        P("req", None, "head"),
        P("req", None),
        P("req"),
        P("req"),
        P("req"),
        P("req", "head"),
        P("head", "req"),
    )
    return jax.shard_map(
        local,
        mesh=mesh,
        in_specs=placed,
        out_specs=(P("req", "head"), P("req", None, "head"), P("req", None, "head")),
        check_vma=False,
    )
```

```python
import math

import jax
import jax.numpy as jnp
from jax import lax
from jax.sharding import Mesh, PartitionSpec as P
from jax.experimental import pallas as pl
from jax.experimental.pallas import tpu as pltpu

HEAD_SIZE = 128


NEGATIVE = -1e30
REQ = ("chip", "core")


def attention_kernel(cached_ref, q_ref, k_ref, v_ref, o_ref, *, fanout, scale_factor):
    member = pl.program_id(0)
    rows = q_ref.shape[0]
    spots = k_ref.shape[0]
    row_ids = lax.broadcasted_iota(jnp.int32, (rows, spots), 0)
    col_ids = lax.broadcasted_iota(jnp.int32, (rows, spots), 1)
    allowed = col_ids <= row_ids + cached_ref[member]
    keys = k_ref[...]
    values = v_ref[...]
    for head in range(fanout):
        lanes = slice(head * HEAD_SIZE, (head + 1) * HEAD_SIZE)
        scores = (
            lax.dot_general(
                q_ref[:, lanes], keys, (((1,), (1,)), ((), ())),
                preferred_element_type=jnp.float32,
            )
            * scale_factor
        )
        scores = jnp.where(allowed, scores, NEGATIVE)
        highest = jnp.max(scores, axis=1, keepdims=True)
        expo_terms = jnp.exp(scores - highest)
        weights = (expo_terms / jnp.sum(expo_terms, axis=1, keepdims=True)).astype(jnp.bfloat16)
        mixed = jnp.dot(weights, values, preferred_element_type=jnp.float32)
        o_ref[:, lanes] = mixed.astype(o_ref.dtype)


def paged_attention(queries, prior_keys, prior_values, cached_lens, fanout, scale_factor):
    per_group, spots, channel_count = prior_keys.shape
    kv_local = channel_count // HEAD_SIZE
    new_limit = queries.shape[0] // per_group
    width = fanout * HEAD_SIZE
    kernel = lambda *refs: attention_kernel(*refs, fanout=fanout, scale_factor=scale_factor)
    return pl.pallas_call(
        kernel,
        grid_spec=pltpu.PrefetchScalarGridSpec(
            num_scalar_prefetch=1,
            grid=(per_group, kv_local),
            in_specs=[
                pl.BlockSpec((new_limit, width), lambda m, g, c: (m, g)),
                pl.BlockSpec((None, spots, HEAD_SIZE), lambda m, g, c: (m, 0, g)),
                pl.BlockSpec((None, spots, HEAD_SIZE), lambda m, g, c: (m, 0, g)),
            ],
            out_specs=pl.BlockSpec((new_limit, width), lambda m, g, c: (m, g)),
        ),
        out_shape=jax.ShapeDtypeStruct(queries.shape, jnp.bfloat16),
        compiler_params=pltpu.CompilerParams(
            dimension_semantics=("arbitrary", "arbitrary"),
        ),
    )(cached_lens, queries, prior_keys, prior_values)


def deal(row_block, new_counts, lead_in, shares, starts, totals, balanced):
    groups = lax.axis_size(REQ)
    my_rank = lax.axis_index(REQ)
    per_group = new_counts.shape[0]
    new_limit = row_block.shape[0] // per_group
    pair_slots = row_block.shape[0] // groups
    columns = row_block.shape[1]
    own_lead = lax.dynamic_index_in_dim(lead_in, my_rank, 0, keepdims=False)
    ordinal = jnp.arange(pair_slots, dtype=jnp.int32)[None, :] * groups + own_lead[:, None]
    ends_at = jnp.cumsum(new_counts)
    request_index = jnp.sum(
        (ordinal[:, :, None] >= ends_at[None, None, :]).astype(jnp.int32), axis=2
    )
    request_index = jnp.minimum(request_index, per_group - 1)
    before = ends_at - new_counts
    source = request_index * new_limit + ordinal - jnp.take(before, request_index)
    own_total = lax.dynamic_index_in_dim(totals, my_rank, 0, keepdims=False)
    is_live = ordinal < own_total
    source = jnp.where(is_live, source, 0)
    picked = jnp.take(row_block, source.reshape(-1), axis=0).reshape(groups, pair_slots, columns)
    outgoing = jnp.where(is_live[:, :, None], picked, jnp.zeros((), row_block.dtype))
    arrived = lax.all_to_all(outgoing, REQ, split_axis=0, concat_axis=0, tiled=True)
    own_shares = lax.dynamic_index_in_dim(shares, my_rank, 1, keepdims=False)
    own_starts = lax.dynamic_index_in_dim(starts, my_rank, 1, keepdims=False)
    within = jnp.arange(pair_slots, dtype=jnp.int32)[None, :]
    landing = jnp.where(within < own_shares[:, None], own_starts[:, None] + within, balanced)
    blank_rows = jnp.zeros((balanced, columns), row_block.dtype)
    return blank_rows.at[landing.reshape(-1)].set(arrived.reshape(-1, columns), mode="drop")


def project_and_sum(row_block, out_weight):
    head_groups = lax.axis_size("head")
    chips = lax.axis_size("chip")
    rows = row_block.shape[0]
    inner, block_cols = out_weight.shape
    weight_part = lax.all_gather(out_weight, "chip", axis=1, tiled=True)
    both_rows = lax.all_gather(row_block, "core", axis=0, tiled=True)
    partial_sum = jnp.dot(both_rows, weight_part, preferred_element_type=jnp.float32)
    per_chunk = chips // head_groups
    partial_sum = partial_sum.astype(jnp.bfloat16).reshape(2 * rows, head_groups, per_chunk * block_cols)
    reduced = lax.psum_scatter(
        jnp.moveaxis(partial_sum, 1, 0), "head", scatter_dimension=0, tiled=True
    ).reshape(2, rows, per_chunk, block_cols)
    arrived = lax.all_to_all(reduced, "core", split_axis=0, concat_axis=0, tiled=True)
    return jnp.moveaxis(arrived, 0, 2).reshape(rows, 2 * per_chunk * block_cols)


def local(
    queries,
    new_keys,
    fresh_values,
    key_page_pool,
    value_page_pool,
    page_table,
    new_counts,
    cached_lens,
    deal_offset,
    residual,
    out_weight,
):
    groups = lax.axis_size(REQ)
    per_group = new_counts.shape[0]
    page_count = page_table.shape[1]
    page_rows = key_page_pool.shape[1]
    channel_count = key_page_pool.shape[2]
    kv_local = channel_count // HEAD_SIZE
    slot_count = queries.shape[0]
    new_limit = slot_count // per_group
    q_width = queries.shape[1]
    group_fanout = q_width // channel_count
    balanced = residual.shape[0]
    new_slot = jnp.arange(new_limit, dtype=jnp.int32)
    positions = cached_lens[:, None] + new_slot[None, :]
    page_of = jnp.take_along_axis(page_table, positions // page_rows, axis=1)
    outside = key_page_pool.shape[0] * page_rows
    target = jnp.where(
        new_slot[None, :] < new_counts[:, None],
        page_of * page_rows + positions % page_rows,
        outside,
    ).reshape(-1)
    flat_keys = key_page_pool.reshape(-1, channel_count).at[target].set(new_keys, mode="drop")
    flat_values = (
        value_page_pool.reshape(-1, channel_count).at[target].set(fresh_values, mode="drop")
    )
    gathered_keys = flat_keys.reshape(key_page_pool.shape)
    gathered_values = flat_values.reshape(value_page_pool.shape)
    scale_factor = 1.0 / math.sqrt(HEAD_SIZE)
    table = page_table
    prior_keys = gathered_keys[table].reshape(per_group, page_count * page_rows, channel_count)
    prior_values = gathered_values[table].reshape(per_group, page_count * page_rows, channel_count)
    attended = paged_attention(
        queries, prior_keys, prior_values, cached_lens, group_fanout, scale_factor
    )
    load_counts, offsets_all = (
        lax.all_gather(new_counts, REQ, axis=0, tiled=True),
        lax.all_gather(deal_offset, REQ, axis=0, tiled=True),
    )
    totals = jnp.sum(load_counts.reshape(groups, per_group), axis=1)
    rank_ids = jnp.arange(groups, dtype=jnp.int32)
    lead_in = jnp.remainder(rank_ids[None, :] - offsets_all[:, None], groups)
    shares = jnp.maximum((totals[:, None] - lead_in + groups - 1) // groups, 0)
    starts = jnp.cumsum(shares, axis=0) - shares
    placed = deal(attended, new_counts, lead_in, shares, starts, totals, balanced)
    summed = project_and_sum(placed, out_weight)
    hidden = (residual.astype(jnp.float32) + summed.astype(jnp.float32)).astype(jnp.bfloat16)
    return (hidden, gathered_keys, gathered_values)


def solution(mesh):
    req_size = mesh.shape["req"]
    split_mesh = Mesh(
        mesh.devices.reshape(req_size // 2, 2, mesh.shape["head"]), ("chip", "core", "head")
    )
    placed = (
        P(REQ, "head"),
        P(REQ, "head"),
        P(REQ, "head"),
        P(REQ, None, "head"),
        P(REQ, None, "head"),
        P(REQ, None),
        P(REQ),
        P(REQ),
        P(REQ),
        P(REQ, "head"),
        P("head", REQ),
    )
    return jax.shard_map(
        local,
        mesh=split_mesh,
        in_specs=placed,
        out_specs=(P(REQ, "head"), P(REQ, None, "head"), P(REQ, None, "head")),
        check_vma=False,
    )
```

```python
import math

import jax
import jax.numpy as jnp
from jax import lax
from jax.sharding import PartitionSpec as P
from jax.experimental import pallas as pl
from jax.experimental.pallas import tpu as pltpu

HEAD_SIZE = 128


NEGATIVE = -1e30


def attention_kernel(cached_ref, q_ref, k_ref, v_ref, o_ref, *, fanout, scale_factor):
    member = pl.program_id(0)
    rows = q_ref.shape[0]
    spots = k_ref.shape[0]
    row_ids = lax.broadcasted_iota(jnp.int32, (rows, spots), 0)
    col_ids = lax.broadcasted_iota(jnp.int32, (rows, spots), 1)
    allowed = col_ids <= row_ids + cached_ref[member]
    keys = k_ref[...]
    values = v_ref[...]
    for head in range(fanout):
        lanes = slice(head * HEAD_SIZE, (head + 1) * HEAD_SIZE)
        scores = (
            lax.dot_general(
                q_ref[:, lanes], keys, (((1,), (1,)), ((), ())),
                preferred_element_type=jnp.float32,
            )
            * scale_factor
        )
        scores = jnp.where(allowed, scores, NEGATIVE)
        highest = jnp.max(scores, axis=1, keepdims=True)
        expo_terms = jnp.exp(scores - highest)
        weights = (expo_terms / jnp.sum(expo_terms, axis=1, keepdims=True)).astype(jnp.bfloat16)
        mixed = jnp.dot(weights, values, preferred_element_type=jnp.float32)
        o_ref[:, lanes] = mixed.astype(o_ref.dtype)


def paged_attention(queries, prior_keys, prior_values, cached_lens, fanout, scale_factor):
    per_group, spots, channel_count = prior_keys.shape
    kv_local = channel_count // HEAD_SIZE
    new_limit = queries.shape[0] // per_group
    width = fanout * HEAD_SIZE
    kernel = lambda *refs: attention_kernel(*refs, fanout=fanout, scale_factor=scale_factor)
    return pl.pallas_call(
        kernel,
        grid_spec=pltpu.PrefetchScalarGridSpec(
            num_scalar_prefetch=1,
            grid=(per_group, kv_local),
            in_specs=[
                pl.BlockSpec((new_limit, width), lambda m, g, c: (m, g)),
                pl.BlockSpec((None, spots, HEAD_SIZE), lambda m, g, c: (m, 0, g)),
                pl.BlockSpec((None, spots, HEAD_SIZE), lambda m, g, c: (m, 0, g)),
            ],
            out_specs=pl.BlockSpec((new_limit, width), lambda m, g, c: (m, g)),
        ),
        out_shape=jax.ShapeDtypeStruct(queries.shape, jnp.bfloat16),
        compiler_params=pltpu.CompilerParams(
            dimension_semantics=("arbitrary", "arbitrary"),
        ),
    )(cached_lens, queries, prior_keys, prior_values)


def deal(row_block, new_counts, lead_in, shares, starts, totals, balanced):
    groups = lax.axis_size("req")
    my_rank = lax.axis_index("req")
    per_group = new_counts.shape[0]
    new_limit = row_block.shape[0] // per_group
    pair_slots = row_block.shape[0] // groups
    columns = row_block.shape[1]
    own_lead = lax.dynamic_index_in_dim(lead_in, my_rank, 0, keepdims=False)
    ordinal = jnp.arange(pair_slots, dtype=jnp.int32)[None, :] * groups + own_lead[:, None]
    ends_at = jnp.cumsum(new_counts)
    request_index = jnp.sum(
        (ordinal[:, :, None] >= ends_at[None, None, :]).astype(jnp.int32), axis=2
    )
    request_index = jnp.minimum(request_index, per_group - 1)
    before = ends_at - new_counts
    source = request_index * new_limit + ordinal - jnp.take(before, request_index)
    own_total = lax.dynamic_index_in_dim(totals, my_rank, 0, keepdims=False)
    is_live = ordinal < own_total
    source = jnp.where(is_live, source, 0)
    picked = jnp.take(row_block, source.reshape(-1), axis=0).reshape(groups, pair_slots, columns)
    outgoing = jnp.where(is_live[:, :, None], picked, jnp.zeros((), row_block.dtype))
    arrived = lax.all_to_all(outgoing, "req", split_axis=0, concat_axis=0, tiled=True)
    own_shares = lax.dynamic_index_in_dim(shares, my_rank, 1, keepdims=False)
    own_starts = lax.dynamic_index_in_dim(starts, my_rank, 1, keepdims=False)
    within = jnp.arange(pair_slots, dtype=jnp.int32)[None, :]
    landing = jnp.where(within < own_shares[:, None], own_starts[:, None] + within, balanced)
    blank_rows = jnp.zeros((balanced, columns), row_block.dtype)
    return blank_rows.at[landing.reshape(-1)].set(arrived.reshape(-1, columns), mode="drop")


def project_and_sum(row_block, out_weight, pieces=2):
    head_groups = lax.axis_size("head")
    groups = lax.axis_size("req")
    rows = row_block.shape[0]
    block_cols = out_weight.shape[1]
    width = block_cols // pieces
    reduced = []
    for piece in range(pieces):
        weight_part = lax.all_gather(
            out_weight[:, piece * width : (piece + 1) * width], "req", axis=1, tiled=True
        )
        partial_sum = jnp.dot(row_block, weight_part, preferred_element_type=jnp.float32)
        summed = lax.psum_scatter(
            partial_sum.astype(jnp.bfloat16), "head", scatter_dimension=1, tiled=True
        )
        reduced.append(summed.reshape(rows, groups // head_groups, width))
    return jnp.stack(reduced, axis=2).reshape(rows, -1)


def local(
    queries,
    new_keys,
    fresh_values,
    key_page_pool,
    value_page_pool,
    page_table,
    new_counts,
    cached_lens,
    deal_offset,
    residual,
    out_weight,
):
    groups = lax.axis_size("req")
    per_group = new_counts.shape[0]
    page_count = page_table.shape[1]
    page_rows = key_page_pool.shape[1]
    channel_count = key_page_pool.shape[2]
    kv_local = channel_count // HEAD_SIZE
    slot_count = queries.shape[0]
    new_limit = slot_count // per_group
    q_width = queries.shape[1]
    group_fanout = q_width // channel_count
    balanced = residual.shape[0]
    new_slot = jnp.arange(new_limit, dtype=jnp.int32)
    positions = cached_lens[:, None] + new_slot[None, :]
    page_of = jnp.take_along_axis(page_table, positions // page_rows, axis=1)
    outside = key_page_pool.shape[0] * page_rows
    target = jnp.where(
        new_slot[None, :] < new_counts[:, None],
        page_of * page_rows + positions % page_rows,
        outside,
    ).reshape(-1)
    flat_keys = key_page_pool.reshape(-1, channel_count).at[target].set(new_keys, mode="drop")
    flat_values = (
        value_page_pool.reshape(-1, channel_count).at[target].set(fresh_values, mode="drop")
    )
    gathered_keys = flat_keys.reshape(key_page_pool.shape)
    gathered_values = flat_values.reshape(value_page_pool.shape)
    scale_factor = 1.0 / math.sqrt(HEAD_SIZE)
    table = page_table
    prior_keys = gathered_keys[table].reshape(per_group, page_count * page_rows, channel_count)
    prior_values = gathered_values[table].reshape(per_group, page_count * page_rows, channel_count)
    attended = paged_attention(
        queries, prior_keys, prior_values, cached_lens, group_fanout, scale_factor
    )
    load_counts, offsets_all = (
        lax.all_gather(new_counts, "req", axis=0, tiled=True),
        lax.all_gather(deal_offset, "req", axis=0, tiled=True),
    )
    totals = jnp.sum(load_counts.reshape(groups, per_group), axis=1)
    rank_ids = jnp.arange(groups, dtype=jnp.int32)
    lead_in = jnp.remainder(rank_ids[None, :] - offsets_all[:, None], groups)
    shares = jnp.maximum((totals[:, None] - lead_in + groups - 1) // groups, 0)
    starts = jnp.cumsum(shares, axis=0) - shares
    placed = deal(attended, new_counts, lead_in, shares, starts, totals, balanced)
    summed = project_and_sum(placed, out_weight)
    hidden = (residual.astype(jnp.float32) + summed.astype(jnp.float32)).astype(jnp.bfloat16)
    return (hidden, gathered_keys, gathered_values)


def solution(mesh):
    placed = (
        P("req", "head"),
        P("req", "head"),
        P("req", "head"),
        P("req", None, "head"),
        P("req", None, "head"),
        P("req", None),
        P("req"),
        P("req"),
        P("req"),
        P("req", "head"),
        P("head", "req"),
    )
    return jax.shard_map(
        local,
        mesh=mesh,
        in_specs=placed,
        out_specs=(P("req", "head"), P("req", None, "head"), P("req", None, "head")),
        check_vma=False,
    )
```

```python
import math

import jax
import jax.numpy as jnp
from jax import lax
from jax.sharding import PartitionSpec as P
from jax.experimental import pallas as pl
from jax.experimental.pallas import tpu as pltpu

HEAD_SIZE = 128


NEGATIVE = -1e30


def attention_kernel(cached_ref, q_ref, k_ref, v_ref, o_ref, *, fanout, scale_factor):
    member = pl.program_id(0)
    rows = q_ref.shape[0]
    spots = k_ref.shape[0]
    row_ids = lax.broadcasted_iota(jnp.int32, (rows, spots), 0)
    col_ids = lax.broadcasted_iota(jnp.int32, (rows, spots), 1)
    allowed = col_ids <= row_ids + cached_ref[member]
    keys = k_ref[...]
    values = v_ref[...]
    for head in range(fanout):
        lanes = slice(head * HEAD_SIZE, (head + 1) * HEAD_SIZE)
        scores = (
            lax.dot_general(
                q_ref[:, lanes], keys, (((1,), (1,)), ((), ())),
                preferred_element_type=jnp.float32,
            )
            * scale_factor
        )
        scores = jnp.where(allowed, scores, NEGATIVE)
        highest = jnp.max(scores, axis=1, keepdims=True)
        expo_terms = jnp.exp(scores - highest)
        weights = (expo_terms / jnp.sum(expo_terms, axis=1, keepdims=True)).astype(jnp.bfloat16)
        mixed = jnp.dot(weights, values, preferred_element_type=jnp.float32)
        o_ref[:, lanes] = mixed.astype(o_ref.dtype)


def paged_attention(queries, prior_keys, prior_values, cached_lens, fanout, scale_factor):
    per_group, spots, channel_count = prior_keys.shape
    kv_local = channel_count // HEAD_SIZE
    new_limit = queries.shape[0] // per_group
    width = fanout * HEAD_SIZE
    kernel = lambda *refs: attention_kernel(*refs, fanout=fanout, scale_factor=scale_factor)
    return pl.pallas_call(
        kernel,
        grid_spec=pltpu.PrefetchScalarGridSpec(
            num_scalar_prefetch=1,
            grid=(per_group, kv_local),
            in_specs=[
                pl.BlockSpec((new_limit, width), lambda m, g, c: (m, g)),
                pl.BlockSpec((None, spots, HEAD_SIZE), lambda m, g, c: (m, 0, g)),
                pl.BlockSpec((None, spots, HEAD_SIZE), lambda m, g, c: (m, 0, g)),
            ],
            out_specs=pl.BlockSpec((new_limit, width), lambda m, g, c: (m, g)),
        ),
        out_shape=jax.ShapeDtypeStruct(queries.shape, jnp.bfloat16),
        compiler_params=pltpu.CompilerParams(
            dimension_semantics=("arbitrary", "arbitrary"),
        ),
    )(cached_lens, queries, prior_keys, prior_values)


def deal(row_block, new_counts, lead_in, shares, starts, totals, balanced):
    groups = lax.axis_size("req")
    my_rank = lax.axis_index("req")
    per_group = new_counts.shape[0]
    new_limit = row_block.shape[0] // per_group
    pair_slots = row_block.shape[0] // groups
    columns = row_block.shape[1]
    own_lead = lax.dynamic_index_in_dim(lead_in, my_rank, 0, keepdims=False)
    ordinal = jnp.arange(pair_slots, dtype=jnp.int32)[None, :] * groups + own_lead[:, None]
    ends_at = jnp.cumsum(new_counts)
    request_index = jnp.sum(
        (ordinal[:, :, None] >= ends_at[None, None, :]).astype(jnp.int32), axis=2
    )
    request_index = jnp.minimum(request_index, per_group - 1)
    before = ends_at - new_counts
    source = request_index * new_limit + ordinal - jnp.take(before, request_index)
    own_total = lax.dynamic_index_in_dim(totals, my_rank, 0, keepdims=False)
    is_live = ordinal < own_total
    source = jnp.where(is_live, source, 0)
    picked = jnp.take(row_block, source.reshape(-1), axis=0).reshape(groups, pair_slots, columns)
    outgoing = jnp.where(is_live[:, :, None], picked, jnp.zeros((), row_block.dtype))
    arrived = lax.all_to_all(outgoing, "req", split_axis=0, concat_axis=0, tiled=True)
    own_shares = lax.dynamic_index_in_dim(shares, my_rank, 1, keepdims=False)
    own_starts = lax.dynamic_index_in_dim(starts, my_rank, 1, keepdims=False)
    within = jnp.arange(pair_slots, dtype=jnp.int32)[None, :]
    landing = jnp.where(within < own_shares[:, None], own_starts[:, None] + within, balanced)
    blank_rows = jnp.zeros((balanced, columns), row_block.dtype)
    return blank_rows.at[landing.reshape(-1)].set(arrived.reshape(-1, columns), mode="drop")


def project(row_block, out_weight):
    blocks = lax.all_gather(out_weight, "req", axis=0, tiled=False)
    product = jnp.einsum("rk,ckn->rcn", row_block, blocks, preferred_element_type=jnp.float32)
    return product.reshape(row_block.shape[0], -1)


def head_total(partial_sum):
    return lax.psum_scatter(
        partial_sum.astype(jnp.bfloat16), "head", scatter_dimension=1, tiled=True
    ).astype(jnp.float32)


def local(
    queries,
    new_keys,
    fresh_values,
    key_page_pool,
    value_page_pool,
    page_table,
    new_counts,
    cached_lens,
    deal_offset,
    residual,
    out_weight,
):
    groups = lax.axis_size("req")
    per_group = new_counts.shape[0]
    page_count = page_table.shape[1]
    page_rows = key_page_pool.shape[1]
    channel_count = key_page_pool.shape[2]
    kv_local = channel_count // HEAD_SIZE
    slot_count = queries.shape[0]
    new_limit = slot_count // per_group
    q_width = queries.shape[1]
    group_fanout = q_width // channel_count
    balanced = residual.shape[0]
    new_slot = jnp.arange(new_limit, dtype=jnp.int32)
    positions = cached_lens[:, None] + new_slot[None, :]
    page_of = jnp.take_along_axis(page_table, positions // page_rows, axis=1)
    outside = key_page_pool.shape[0] * page_rows
    target = jnp.where(
        new_slot[None, :] < new_counts[:, None],
        page_of * page_rows + positions % page_rows,
        outside,
    ).reshape(-1)
    flat_keys = key_page_pool.reshape(-1, channel_count).at[target].set(new_keys, mode="drop")
    flat_values = (
        value_page_pool.reshape(-1, channel_count).at[target].set(fresh_values, mode="drop")
    )
    gathered_keys = flat_keys.reshape(key_page_pool.shape)
    gathered_values = flat_values.reshape(value_page_pool.shape)
    scale_factor = 1.0 / math.sqrt(HEAD_SIZE)
    table = page_table
    prior_keys = gathered_keys[table].reshape(per_group, page_count * page_rows, channel_count)
    prior_values = gathered_values[table].reshape(per_group, page_count * page_rows, channel_count)
    attended = paged_attention(
        queries, prior_keys, prior_values, cached_lens, group_fanout, scale_factor
    )
    load_counts, offsets_all = (
        lax.all_gather(new_counts, "req", axis=0, tiled=True),
        lax.all_gather(deal_offset, "req", axis=0, tiled=True),
    )
    totals = jnp.sum(load_counts.reshape(groups, per_group), axis=1)
    rank_ids = jnp.arange(groups, dtype=jnp.int32)
    lead_in = jnp.remainder(rank_ids[None, :] - offsets_all[:, None], groups)
    shares = jnp.maximum((totals[:, None] - lead_in + groups - 1) // groups, 0)
    starts = jnp.cumsum(shares, axis=0) - shares
    placed = deal(attended, new_counts, lead_in, shares, starts, totals, balanced)
    summed = head_total(project(placed, out_weight)).astype(jnp.bfloat16)
    hidden = (residual.astype(jnp.float32) + summed.astype(jnp.float32)).astype(jnp.bfloat16)
    return (hidden, gathered_keys, gathered_values)


def solution(mesh):
    placed = (
        P("req", "head"),
        P("req", "head"),
        P("req", "head"),
        P("req", None, "head"),
        P("req", None, "head"),
        P("req", None),
        P("req"),
        P("req"),
        P("req"),
        P("req", "head"),
        P("head", "req"),
    )
    return jax.shard_map(
        local,
        mesh=mesh,
        in_specs=placed,
        out_specs=(P("req", "head"), P("req", None, "head"), P("req", None, "head")),
        check_vma=False,
    )
```

```python
import math

import jax
import jax.numpy as jnp
from jax import lax
from jax.sharding import Mesh, PartitionSpec as P
from jax.experimental import pallas as pl
from jax.experimental.pallas import tpu as pltpu

HEAD_SIZE = 128


NEGATIVE = -1e30
REQ = ("y", "x", "core")


def attention_kernel(cached_ref, q_ref, k_ref, v_ref, o_ref, *, fanout, scale_factor):
    member = pl.program_id(0)
    rows = q_ref.shape[0]
    spots = k_ref.shape[0]
    row_ids = lax.broadcasted_iota(jnp.int32, (rows, spots), 0)
    col_ids = lax.broadcasted_iota(jnp.int32, (rows, spots), 1)
    allowed = col_ids <= row_ids + cached_ref[member]
    keys = k_ref[...]
    values = v_ref[...]
    for head in range(fanout):
        lanes = slice(head * HEAD_SIZE, (head + 1) * HEAD_SIZE)
        scores = (
            lax.dot_general(
                q_ref[:, lanes], keys, (((1,), (1,)), ((), ())),
                preferred_element_type=jnp.float32,
            )
            * scale_factor
        )
        scores = jnp.where(allowed, scores, NEGATIVE)
        highest = jnp.max(scores, axis=1, keepdims=True)
        expo_terms = jnp.exp(scores - highest)
        weights = (expo_terms / jnp.sum(expo_terms, axis=1, keepdims=True)).astype(jnp.bfloat16)
        mixed = jnp.dot(weights, values, preferred_element_type=jnp.float32)
        o_ref[:, lanes] = mixed.astype(o_ref.dtype)


def paged_attention(queries, prior_keys, prior_values, cached_lens, fanout, scale_factor):
    per_group, spots, channel_count = prior_keys.shape
    kv_local = channel_count // HEAD_SIZE
    new_limit = queries.shape[0] // per_group
    width = fanout * HEAD_SIZE
    kernel = lambda *refs: attention_kernel(*refs, fanout=fanout, scale_factor=scale_factor)
    return pl.pallas_call(
        kernel,
        grid_spec=pltpu.PrefetchScalarGridSpec(
            num_scalar_prefetch=1,
            grid=(per_group, kv_local),
            in_specs=[
                pl.BlockSpec((new_limit, width), lambda m, g, c: (m, g)),
                pl.BlockSpec((None, spots, HEAD_SIZE), lambda m, g, c: (m, 0, g)),
                pl.BlockSpec((None, spots, HEAD_SIZE), lambda m, g, c: (m, 0, g)),
            ],
            out_specs=pl.BlockSpec((new_limit, width), lambda m, g, c: (m, g)),
        ),
        out_shape=jax.ShapeDtypeStruct(queries.shape, jnp.bfloat16),
        compiler_params=pltpu.CompilerParams(
            dimension_semantics=("arbitrary", "arbitrary"),
        ),
    )(cached_lens, queries, prior_keys, prior_values)


def deal(row_block, new_counts, lead_in, shares, starts, totals, balanced):
    groups = lax.axis_size(REQ)
    my_rank = lax.axis_index(REQ)
    per_group = new_counts.shape[0]
    new_limit = row_block.shape[0] // per_group
    pair_slots = row_block.shape[0] // groups
    columns = row_block.shape[1]
    own_lead = lax.dynamic_index_in_dim(lead_in, my_rank, 0, keepdims=False)
    ordinal = jnp.arange(pair_slots, dtype=jnp.int32)[None, :] * groups + own_lead[:, None]
    ends_at = jnp.cumsum(new_counts)
    request_index = jnp.sum(
        (ordinal[:, :, None] >= ends_at[None, None, :]).astype(jnp.int32), axis=2
    )
    request_index = jnp.minimum(request_index, per_group - 1)
    before = ends_at - new_counts
    source = request_index * new_limit + ordinal - jnp.take(before, request_index)
    own_total = lax.dynamic_index_in_dim(totals, my_rank, 0, keepdims=False)
    is_live = ordinal < own_total
    source = jnp.where(is_live, source, 0)
    picked = jnp.take(row_block, source.reshape(-1), axis=0).reshape(groups, pair_slots, columns)
    outgoing = jnp.where(is_live[:, :, None], picked, jnp.zeros((), row_block.dtype))
    arrived = lax.all_to_all(outgoing, REQ, split_axis=0, concat_axis=0, tiled=True)
    own_shares = lax.dynamic_index_in_dim(shares, my_rank, 1, keepdims=False)
    own_starts = lax.dynamic_index_in_dim(starts, my_rank, 1, keepdims=False)
    within = jnp.arange(pair_slots, dtype=jnp.int32)[None, :]
    landing = jnp.where(within < own_shares[:, None], own_starts[:, None] + within, balanced)
    blank_rows = jnp.zeros((balanced, columns), row_block.dtype)
    return blank_rows.at[landing.reshape(-1)].set(arrived.reshape(-1, columns), mode="drop")


def project_and_sum(row_block, out_weight):
    head_groups = lax.axis_size("head")
    chips = lax.axis_size("y") * lax.axis_size("x")
    rows = row_block.shape[0]
    inner = out_weight.shape[0]
    block_cols = out_weight.shape[1] // chips
    weight_part = out_weight
    both_rows = lax.all_gather(row_block, "core", axis=0, tiled=True)
    partial_sum = jnp.dot(both_rows, weight_part, preferred_element_type=jnp.float32)
    per_chunk = chips // head_groups
    partial_sum = partial_sum.astype(jnp.bfloat16).reshape(2 * rows, head_groups, per_chunk * block_cols)
    reduced = lax.psum_scatter(
        jnp.moveaxis(partial_sum, 1, 0), "head", scatter_dimension=0, tiled=True
    ).reshape(2, rows, per_chunk, block_cols)
    arrived = lax.all_to_all(reduced, "core", split_axis=0, concat_axis=0, tiled=True)
    return jnp.moveaxis(arrived, 0, 2).reshape(rows, 2 * per_chunk * block_cols)


def local(
    queries,
    new_keys,
    fresh_values,
    key_page_pool,
    value_page_pool,
    page_table,
    new_counts,
    cached_lens,
    deal_offset,
    residual,
    out_weight,
):
    groups = lax.axis_size(REQ)
    per_group = new_counts.shape[0]
    page_count = page_table.shape[1]
    page_rows = key_page_pool.shape[1]
    channel_count = key_page_pool.shape[2]
    kv_local = channel_count // HEAD_SIZE
    slot_count = queries.shape[0]
    new_limit = slot_count // per_group
    q_width = queries.shape[1]
    group_fanout = q_width // channel_count
    balanced = residual.shape[0]
    new_slot = jnp.arange(new_limit, dtype=jnp.int32)
    positions = cached_lens[:, None] + new_slot[None, :]
    page_of = jnp.take_along_axis(page_table, positions // page_rows, axis=1)
    outside = key_page_pool.shape[0] * page_rows
    target = jnp.where(
        new_slot[None, :] < new_counts[:, None],
        page_of * page_rows + positions % page_rows,
        outside,
    ).reshape(-1)
    flat_keys = key_page_pool.reshape(-1, channel_count).at[target].set(new_keys, mode="drop")
    flat_values = (
        value_page_pool.reshape(-1, channel_count).at[target].set(fresh_values, mode="drop")
    )
    gathered_keys = flat_keys.reshape(key_page_pool.shape)
    gathered_values = flat_values.reshape(value_page_pool.shape)
    scale_factor = 1.0 / math.sqrt(HEAD_SIZE)
    table = page_table
    prior_keys = gathered_keys[table].reshape(per_group, page_count * page_rows, channel_count)
    prior_values = gathered_values[table].reshape(per_group, page_count * page_rows, channel_count)
    attended = paged_attention(
        queries, prior_keys, prior_values, cached_lens, group_fanout, scale_factor
    )
    load_counts, offsets_all = (
        lax.all_gather(new_counts, REQ, axis=0, tiled=True),
        lax.all_gather(deal_offset, REQ, axis=0, tiled=True),
    )
    totals = jnp.sum(load_counts.reshape(groups, per_group), axis=1)
    rank_ids = jnp.arange(groups, dtype=jnp.int32)
    lead_in = jnp.remainder(rank_ids[None, :] - offsets_all[:, None], groups)
    shares = jnp.maximum((totals[:, None] - lead_in + groups - 1) // groups, 0)
    starts = jnp.cumsum(shares, axis=0) - shares
    weight_near = lax.all_gather(out_weight, "x", axis=1, tiled=True)
    weight_near = lax.all_gather(weight_near, "y", axis=1, tiled=True)
    weight_near, attended = lax.optimization_barrier((weight_near, attended))
    placed = deal(attended, new_counts, lead_in, shares, starts, totals, balanced)
    summed = project_and_sum(placed, weight_near)
    hidden = (residual.astype(jnp.float32) + summed.astype(jnp.float32)).astype(jnp.bfloat16)
    return (hidden, gathered_keys, gathered_values)


def solution(mesh):
    req_size = mesh.shape["req"]
    side = math.isqrt(req_size // 2)
    split_mesh = Mesh(
        mesh.devices.reshape(req_size // 2 // side, side, 2, mesh.shape["head"]),
        ("y", "x", "core", "head"),
    )
    placed = (
        P(REQ, "head"),
        P(REQ, "head"),
        P(REQ, "head"),
        P(REQ, None, "head"),
        P(REQ, None, "head"),
        P(REQ, None),
        P(REQ),
        P(REQ),
        P(REQ),
        P(REQ, "head"),
        P("head", REQ),
    )
    return jax.shard_map(
        local,
        mesh=split_mesh,
        in_specs=placed,
        out_specs=(P(REQ, "head"), P(REQ, None, "head"), P(REQ, None, "head")),
        check_vma=False,
    )
```

```python
import math

import jax
import jax.numpy as jnp
from jax import lax
from jax.sharding import PartitionSpec as P
from jax.experimental import pallas as pl
from jax.experimental.pallas import tpu as pltpu

HEAD_SIZE = 128


NEGATIVE = -1e30


def attention_kernel(cached_ref, q_ref, k_ref, v_ref, o_ref, *, fanout, scale_factor):
    member = pl.program_id(0)
    rows = q_ref.shape[0]
    spots = k_ref.shape[0]
    row_ids = lax.broadcasted_iota(jnp.int32, (rows, spots), 0)
    col_ids = lax.broadcasted_iota(jnp.int32, (rows, spots), 1)
    allowed = col_ids <= row_ids + cached_ref[member]
    keys = k_ref[...]
    values = v_ref[...]
    for head in range(fanout):
        lanes = slice(head * HEAD_SIZE, (head + 1) * HEAD_SIZE)
        scores = (
            lax.dot_general(
                q_ref[:, lanes], keys, (((1,), (1,)), ((), ())),
                preferred_element_type=jnp.float32,
            )
            * scale_factor
        )
        scores = jnp.where(allowed, scores, NEGATIVE)
        highest = jnp.max(scores, axis=1, keepdims=True)
        expo_terms = jnp.exp(scores - highest)
        weights = (expo_terms / jnp.sum(expo_terms, axis=1, keepdims=True)).astype(jnp.bfloat16)
        mixed = jnp.dot(weights, values, preferred_element_type=jnp.float32)
        o_ref[:, lanes] = mixed.astype(o_ref.dtype)


def paged_attention(queries, prior_keys, prior_values, cached_lens, fanout, scale_factor):
    per_group, spots, channel_count = prior_keys.shape
    kv_local = channel_count // HEAD_SIZE
    new_limit = queries.shape[0] // per_group
    width = fanout * HEAD_SIZE
    kernel = lambda *refs: attention_kernel(*refs, fanout=fanout, scale_factor=scale_factor)
    return pl.pallas_call(
        kernel,
        grid_spec=pltpu.PrefetchScalarGridSpec(
            num_scalar_prefetch=1,
            grid=(per_group, kv_local),
            in_specs=[
                pl.BlockSpec((new_limit, width), lambda m, g, c: (m, g)),
                pl.BlockSpec((None, spots, HEAD_SIZE), lambda m, g, c: (m, 0, g)),
                pl.BlockSpec((None, spots, HEAD_SIZE), lambda m, g, c: (m, 0, g)),
            ],
            out_specs=pl.BlockSpec((new_limit, width), lambda m, g, c: (m, g)),
        ),
        out_shape=jax.ShapeDtypeStruct(queries.shape, jnp.bfloat16),
        compiler_params=pltpu.CompilerParams(
            dimension_semantics=("arbitrary", "arbitrary"),
        ),
    )(cached_lens, queries, prior_keys, prior_values)


def deal(row_block, new_counts, lead_in, shares, starts, totals, balanced):
    groups = lax.axis_size("req")
    my_rank = lax.axis_index("req")
    per_group = new_counts.shape[0]
    new_limit = row_block.shape[0] // per_group
    pair_slots = row_block.shape[0] // groups
    columns = row_block.shape[1]
    own_lead = lax.dynamic_index_in_dim(lead_in, my_rank, 0, keepdims=False)
    ordinal = jnp.arange(pair_slots, dtype=jnp.int32)[None, :] * groups + own_lead[:, None]
    ends_at = jnp.cumsum(new_counts)
    request_index = jnp.sum(
        (ordinal[:, :, None] >= ends_at[None, None, :]).astype(jnp.int32), axis=2
    )
    request_index = jnp.minimum(request_index, per_group - 1)
    before = ends_at - new_counts
    source = request_index * new_limit + ordinal - jnp.take(before, request_index)
    own_total = lax.dynamic_index_in_dim(totals, my_rank, 0, keepdims=False)
    is_live = ordinal < own_total
    source = jnp.where(is_live, source, 0)
    picked = jnp.take(row_block, source.reshape(-1), axis=0).reshape(groups, pair_slots, columns)
    outgoing = jnp.where(is_live[:, :, None], picked, jnp.zeros((), row_block.dtype))
    arrived = lax.all_to_all(outgoing, "req", split_axis=0, concat_axis=0, tiled=True)
    own_shares = lax.dynamic_index_in_dim(shares, my_rank, 1, keepdims=False)
    own_starts = lax.dynamic_index_in_dim(starts, my_rank, 1, keepdims=False)
    within = jnp.arange(pair_slots, dtype=jnp.int32)[None, :]
    landing = jnp.where(within < own_shares[:, None], own_starts[:, None] + within, balanced)
    blank_rows = jnp.zeros((balanced, columns), row_block.dtype)
    return blank_rows.at[landing.reshape(-1)].set(arrived.reshape(-1, columns), mode="drop")


def project(row_block, out_weight):
    return jnp.dot(
        row_block,
        lax.all_gather(out_weight, "req", axis=1, tiled=True),
        preferred_element_type=jnp.float32,
    )


def head_total(partial_sum):
    head_groups = lax.axis_size("head")
    rows, columns = partial_sum.shape
    terms = partial_sum.astype(jnp.bfloat16).reshape(rows, head_groups, columns // head_groups)
    arrived = lax.all_to_all(
        jnp.moveaxis(terms, 1, 0), "head", split_axis=0, concat_axis=0, tiled=True
    )
    return jnp.sum(arrived.astype(jnp.float32), axis=0)


def local(
    queries,
    new_keys,
    fresh_values,
    key_page_pool,
    value_page_pool,
    page_table,
    new_counts,
    cached_lens,
    deal_offset,
    residual,
    out_weight,
):
    groups = lax.axis_size("req")
    per_group = new_counts.shape[0]
    page_count = page_table.shape[1]
    page_rows = key_page_pool.shape[1]
    channel_count = key_page_pool.shape[2]
    kv_local = channel_count // HEAD_SIZE
    slot_count = queries.shape[0]
    new_limit = slot_count // per_group
    q_width = queries.shape[1]
    group_fanout = q_width // channel_count
    balanced = residual.shape[0]
    new_slot = jnp.arange(new_limit, dtype=jnp.int32)
    positions = cached_lens[:, None] + new_slot[None, :]
    page_of = jnp.take_along_axis(page_table, positions // page_rows, axis=1)
    outside = key_page_pool.shape[0] * page_rows
    target = jnp.where(
        new_slot[None, :] < new_counts[:, None],
        page_of * page_rows + positions % page_rows,
        outside,
    ).reshape(-1)
    flat_keys = key_page_pool.reshape(-1, channel_count).at[target].set(new_keys, mode="drop")
    flat_values = (
        value_page_pool.reshape(-1, channel_count).at[target].set(fresh_values, mode="drop")
    )
    gathered_keys = flat_keys.reshape(key_page_pool.shape)
    gathered_values = flat_values.reshape(value_page_pool.shape)
    scale_factor = 1.0 / math.sqrt(HEAD_SIZE)
    table = page_table
    prior_keys = gathered_keys[table].reshape(per_group, page_count * page_rows, channel_count)
    prior_values = gathered_values[table].reshape(per_group, page_count * page_rows, channel_count)
    attended = paged_attention(
        queries, prior_keys, prior_values, cached_lens, group_fanout, scale_factor
    )
    load_counts, offsets_all = (
        lax.all_gather(new_counts, "req", axis=0, tiled=True),
        lax.all_gather(deal_offset, "req", axis=0, tiled=True),
    )
    totals = jnp.sum(load_counts.reshape(groups, per_group), axis=1)
    rank_ids = jnp.arange(groups, dtype=jnp.int32)
    lead_in = jnp.remainder(rank_ids[None, :] - offsets_all[:, None], groups)
    shares = jnp.maximum((totals[:, None] - lead_in + groups - 1) // groups, 0)
    starts = jnp.cumsum(shares, axis=0) - shares
    placed = deal(attended, new_counts, lead_in, shares, starts, totals, balanced)
    summed = head_total(project(placed, out_weight)).astype(jnp.bfloat16)
    hidden = (residual.astype(jnp.float32) + summed.astype(jnp.float32)).astype(jnp.bfloat16)
    return (hidden, gathered_keys, gathered_values)


def solution(mesh):
    placed = (
        P("req", "head"),
        P("req", "head"),
        P("req", "head"),
        P("req", None, "head"),
        P("req", None, "head"),
        P("req", None),
        P("req"),
        P("req"),
        P("req"),
        P("req", "head"),
        P("head", "req"),
    )
    return jax.shard_map(
        local,
        mesh=mesh,
        in_specs=placed,
        out_specs=(P("req", "head"), P("req", None, "head"), P("req", None, "head")),
        check_vma=False,
    )
```

```python
import math

import jax
import jax.numpy as jnp
from jax import lax
from jax.sharding import PartitionSpec as P
from jax.experimental import pallas as pl
from jax.experimental.pallas import tpu as pltpu

HEAD_SIZE = 128


NEGATIVE = -1e30


def attention_kernel(cached_ref, q_ref, k_ref, v_ref, o_ref, *, fanout, scale_factor):
    member = pl.program_id(0)
    rows = q_ref.shape[0]
    spots = k_ref.shape[0]
    row_ids = lax.broadcasted_iota(jnp.int32, (rows, spots), 0)
    col_ids = lax.broadcasted_iota(jnp.int32, (rows, spots), 1)
    allowed = col_ids <= row_ids + cached_ref[member]
    keys = k_ref[...]
    values = v_ref[...]
    for head in range(fanout):
        lanes = slice(head * HEAD_SIZE, (head + 1) * HEAD_SIZE)
        scores = (
            lax.dot_general(
                q_ref[:, lanes], keys, (((1,), (1,)), ((), ())),
                preferred_element_type=jnp.float32,
            )
            * scale_factor
        )
        scores = jnp.where(allowed, scores, NEGATIVE)
        highest = jnp.max(scores, axis=1, keepdims=True)
        expo_terms = jnp.exp(scores - highest)
        weights = (expo_terms / jnp.sum(expo_terms, axis=1, keepdims=True)).astype(jnp.bfloat16)
        mixed = jnp.dot(weights, values, preferred_element_type=jnp.float32)
        o_ref[:, lanes] = mixed.astype(o_ref.dtype)


def paged_attention(queries, prior_keys, prior_values, cached_lens, fanout, scale_factor):
    per_group, spots, channel_count = prior_keys.shape
    kv_local = channel_count // HEAD_SIZE
    new_limit = queries.shape[0] // per_group
    width = fanout * HEAD_SIZE
    kernel = lambda *refs: attention_kernel(*refs, fanout=fanout, scale_factor=scale_factor)
    return pl.pallas_call(
        kernel,
        grid_spec=pltpu.PrefetchScalarGridSpec(
            num_scalar_prefetch=1,
            grid=(per_group, kv_local),
            in_specs=[
                pl.BlockSpec((new_limit, width), lambda m, g, c: (m, g)),
                pl.BlockSpec((None, spots, HEAD_SIZE), lambda m, g, c: (m, 0, g)),
                pl.BlockSpec((None, spots, HEAD_SIZE), lambda m, g, c: (m, 0, g)),
            ],
            out_specs=pl.BlockSpec((new_limit, width), lambda m, g, c: (m, g)),
        ),
        out_shape=jax.ShapeDtypeStruct(queries.shape, jnp.bfloat16),
        compiler_params=pltpu.CompilerParams(
            dimension_semantics=("arbitrary", "arbitrary"),
        ),
    )(cached_lens, queries, prior_keys, prior_values)


def deal(row_block, new_counts, lead_in, shares, starts, totals, balanced):
    groups = lax.axis_size("req")
    my_rank = lax.axis_index("req")
    per_group = new_counts.shape[0]
    new_limit = row_block.shape[0] // per_group
    pair_slots = row_block.shape[0] // groups
    columns = row_block.shape[1]
    own_lead = lax.dynamic_index_in_dim(lead_in, my_rank, 0, keepdims=False)
    ordinal = jnp.arange(pair_slots, dtype=jnp.int32)[None, :] * groups + own_lead[:, None]
    ends_at = jnp.cumsum(new_counts)
    request_index = jnp.sum(
        (ordinal[:, :, None] >= ends_at[None, None, :]).astype(jnp.int32), axis=2
    )
    request_index = jnp.minimum(request_index, per_group - 1)
    before = ends_at - new_counts
    source = request_index * new_limit + ordinal - jnp.take(before, request_index)
    own_total = lax.dynamic_index_in_dim(totals, my_rank, 0, keepdims=False)
    is_live = ordinal < own_total
    source = jnp.where(is_live, source, 0)
    picked = jnp.take(row_block, source.reshape(-1), axis=0).reshape(groups, pair_slots, columns)
    outgoing = jnp.where(is_live[:, :, None], picked, jnp.zeros((), row_block.dtype))
    arrived = lax.all_to_all(outgoing, "req", split_axis=0, concat_axis=0, tiled=True)
    own_shares = lax.dynamic_index_in_dim(shares, my_rank, 1, keepdims=False)
    own_starts = lax.dynamic_index_in_dim(starts, my_rank, 1, keepdims=False)
    within = jnp.arange(pair_slots, dtype=jnp.int32)[None, :]
    landing = jnp.where(within < own_shares[:, None], own_starts[:, None] + within, balanced)
    blank_rows = jnp.zeros((balanced, columns), row_block.dtype)
    return blank_rows.at[landing.reshape(-1)].set(arrived.reshape(-1, columns), mode="drop")


def head_total(partial_sum):
    return lax.psum_scatter(
        partial_sum.astype(jnp.bfloat16), "head", scatter_dimension=1, tiled=True
    ).astype(jnp.float32)


def local(
    queries,
    new_keys,
    fresh_values,
    key_page_pool,
    value_page_pool,
    page_table,
    new_counts,
    cached_lens,
    deal_offset,
    residual,
    out_weight,
):
    groups = lax.axis_size("req")
    per_group = new_counts.shape[0]
    page_count = page_table.shape[1]
    page_rows = key_page_pool.shape[1]
    channel_count = key_page_pool.shape[2]
    kv_local = channel_count // HEAD_SIZE
    slot_count = queries.shape[0]
    new_limit = slot_count // per_group
    q_width = queries.shape[1]
    group_fanout = q_width // channel_count
    balanced = residual.shape[0]
    new_slot = jnp.arange(new_limit, dtype=jnp.int32)
    positions = cached_lens[:, None] + new_slot[None, :]
    page_of = jnp.take_along_axis(page_table, positions // page_rows, axis=1)
    outside = key_page_pool.shape[0] * page_rows
    target = jnp.where(
        new_slot[None, :] < new_counts[:, None],
        page_of * page_rows + positions % page_rows,
        outside,
    ).reshape(-1)
    flat_keys = key_page_pool.reshape(-1, channel_count).at[target].set(new_keys, mode="drop")
    flat_values = (
        value_page_pool.reshape(-1, channel_count).at[target].set(fresh_values, mode="drop")
    )
    gathered_keys = flat_keys.reshape(key_page_pool.shape)
    gathered_values = flat_values.reshape(value_page_pool.shape)
    scale_factor = 1.0 / math.sqrt(HEAD_SIZE)
    table = page_table
    prior_keys = gathered_keys[table].reshape(per_group, page_count * page_rows, channel_count)
    prior_values = gathered_values[table].reshape(per_group, page_count * page_rows, channel_count)
    attended = paged_attention(
        queries, prior_keys, prior_values, cached_lens, group_fanout, scale_factor
    )
    load_counts, offsets_all = (
        lax.all_gather(new_counts, "req", axis=0, tiled=True),
        lax.all_gather(deal_offset, "req", axis=0, tiled=True),
    )
    totals = jnp.sum(load_counts.reshape(groups, per_group), axis=1)
    rank_ids = jnp.arange(groups, dtype=jnp.int32)
    lead_in = jnp.remainder(rank_ids[None, :] - offsets_all[:, None], groups)
    shares = jnp.maximum((totals[:, None] - lead_in + groups - 1) // groups, 0)
    starts = jnp.cumsum(shares, axis=0) - shares
    placed = deal(attended, new_counts, lead_in, shares, starts, totals, balanced)
    weight_all = lax.all_gather(out_weight, "req", axis=1, tiled=True)
    lead_rows = 40
    summed = jnp.concatenate(
        [
            head_total(jnp.dot(piece, weight_all, preferred_element_type=jnp.float32))
            for piece in (placed[:lead_rows], placed[lead_rows:])
        ]
    ).astype(jnp.bfloat16)
    hidden = (residual.astype(jnp.float32) + summed.astype(jnp.float32)).astype(jnp.bfloat16)
    return (hidden, gathered_keys, gathered_values)


def solution(mesh):
    placed = (
        P("req", "head"),
        P("req", "head"),
        P("req", "head"),
        P("req", None, "head"),
        P("req", None, "head"),
        P("req", None),
        P("req"),
        P("req"),
        P("req"),
        P("req", "head"),
        P("head", "req"),
    )
    return jax.shard_map(
        local,
        mesh=mesh,
        in_specs=placed,
        out_specs=(P("req", "head"), P("req", None, "head"), P("req", None, "head")),
        check_vma=False,
    )
```

```python
import math

import jax
import jax.numpy as jnp
from jax import lax
from jax.sharding import PartitionSpec as P
from jax.experimental import pallas as pl
from jax.experimental.pallas import tpu as pltpu

HEAD_SIZE = 128


NEGATIVE = -1e30


def attention_kernel(cached_ref, q_ref, k_ref, v_ref, o_ref, *, fanout, scale_factor):
    member = pl.program_id(0)
    rows = q_ref.shape[0]
    spots = k_ref.shape[0]
    row_ids = lax.broadcasted_iota(jnp.int32, (rows, spots), 0)
    col_ids = lax.broadcasted_iota(jnp.int32, (rows, spots), 1)
    allowed = col_ids <= row_ids + cached_ref[member]
    keys = k_ref[...]
    values = v_ref[...]
    for head in range(fanout):
        lanes = slice(head * HEAD_SIZE, (head + 1) * HEAD_SIZE)
        scores = (
            lax.dot_general(
                q_ref[:, lanes], keys, (((1,), (1,)), ((), ())),
                preferred_element_type=jnp.float32,
            )
            * scale_factor
        )
        scores = jnp.where(allowed, scores, NEGATIVE)
        highest = jnp.max(scores, axis=1, keepdims=True)
        expo_terms = jnp.exp(scores - highest)
        weights = (expo_terms / jnp.sum(expo_terms, axis=1, keepdims=True)).astype(jnp.bfloat16)
        mixed = jnp.dot(weights, values, preferred_element_type=jnp.float32)
        o_ref[:, lanes] = mixed.astype(o_ref.dtype)


def paged_attention(queries, prior_keys, prior_values, cached_lens, fanout, scale_factor):
    per_group, spots, channel_count = prior_keys.shape
    kv_local = channel_count // HEAD_SIZE
    new_limit = queries.shape[0] // per_group
    width = fanout * HEAD_SIZE
    kernel = lambda *refs: attention_kernel(*refs, fanout=fanout, scale_factor=scale_factor)
    return pl.pallas_call(
        kernel,
        grid_spec=pltpu.PrefetchScalarGridSpec(
            num_scalar_prefetch=1,
            grid=(per_group, kv_local),
            in_specs=[
                pl.BlockSpec((new_limit, width), lambda m, g, c: (m, g)),
                pl.BlockSpec((None, spots, HEAD_SIZE), lambda m, g, c: (m, 0, g)),
                pl.BlockSpec((None, spots, HEAD_SIZE), lambda m, g, c: (m, 0, g)),
            ],
            out_specs=pl.BlockSpec((new_limit, width), lambda m, g, c: (m, g)),
        ),
        out_shape=jax.ShapeDtypeStruct(queries.shape, jnp.bfloat16),
        compiler_params=pltpu.CompilerParams(
            dimension_semantics=("arbitrary", "arbitrary"),
        ),
    )(cached_lens, queries, prior_keys, prior_values)


def deal(row_block, new_counts, lead_in, shares, starts, totals, balanced):
    groups = lax.axis_size("req")
    my_rank = lax.axis_index("req")
    per_group = new_counts.shape[0]
    new_limit = row_block.shape[0] // per_group
    pair_slots = row_block.shape[0] // groups
    columns = row_block.shape[1]
    own_lead = lax.dynamic_index_in_dim(lead_in, my_rank, 0, keepdims=False)
    ordinal = jnp.arange(pair_slots, dtype=jnp.int32)[None, :] * groups + own_lead[:, None]
    ends_at = jnp.cumsum(new_counts)
    request_index = jnp.sum(
        (ordinal[:, :, None] >= ends_at[None, None, :]).astype(jnp.int32), axis=2
    )
    request_index = jnp.minimum(request_index, per_group - 1)
    before = ends_at - new_counts
    source = request_index * new_limit + ordinal - jnp.take(before, request_index)
    own_total = lax.dynamic_index_in_dim(totals, my_rank, 0, keepdims=False)
    is_live = ordinal < own_total
    source = jnp.where(is_live, source, 0)
    picked = jnp.take(row_block, source.reshape(-1), axis=0).reshape(groups, pair_slots, columns)
    outgoing = jnp.where(is_live[:, :, None], picked, jnp.zeros((), row_block.dtype))
    arrived = lax.all_to_all(outgoing, "req", split_axis=0, concat_axis=0, tiled=True)
    own_shares = lax.dynamic_index_in_dim(shares, my_rank, 1, keepdims=False)
    own_starts = lax.dynamic_index_in_dim(starts, my_rank, 1, keepdims=False)
    within = jnp.arange(pair_slots, dtype=jnp.int32)[None, :]
    landing = jnp.where(within < own_shares[:, None], own_starts[:, None] + within, balanced)
    blank_rows = jnp.zeros((balanced, columns), row_block.dtype)
    return blank_rows.at[landing.reshape(-1)].set(arrived.reshape(-1, columns), mode="drop")


def project(row_block, out_weight):
    return jnp.dot(
        row_block,
        lax.all_gather(out_weight, "req", axis=1, tiled=True),
        preferred_element_type=jnp.float32,
    )


def head_total(partial_sum):
    return lax.psum_scatter(
        partial_sum.astype(jnp.bfloat16), "head", scatter_dimension=1, tiled=True
    ).astype(jnp.float32)


def local(
    queries,
    new_keys,
    fresh_values,
    key_page_pool,
    value_page_pool,
    page_table,
    new_counts,
    cached_lens,
    deal_offset,
    residual,
    out_weight,
):
    groups = lax.axis_size("req")
    per_group = new_counts.shape[0]
    page_count = page_table.shape[1]
    page_rows = key_page_pool.shape[1]
    channel_count = key_page_pool.shape[2]
    kv_local = channel_count // HEAD_SIZE
    slot_count = queries.shape[0]
    new_limit = slot_count // per_group
    q_width = queries.shape[1]
    group_fanout = q_width // channel_count
    balanced = residual.shape[0]
    new_slot = jnp.arange(new_limit, dtype=jnp.int32)
    positions = cached_lens[:, None] + new_slot[None, :]
    page_of = jnp.take_along_axis(page_table, positions // page_rows, axis=1)
    outside = key_page_pool.shape[0] * page_rows
    target = jnp.where(
        new_slot[None, :] < new_counts[:, None],
        page_of * page_rows + positions % page_rows,
        outside,
    ).reshape(-1)
    flat_keys = key_page_pool.reshape(-1, channel_count).at[target].set(new_keys, mode="drop")
    flat_values = (
        value_page_pool.reshape(-1, channel_count).at[target].set(fresh_values, mode="drop")
    )
    gathered_keys = flat_keys.reshape(key_page_pool.shape)
    gathered_values = flat_values.reshape(value_page_pool.shape)
    scale_factor = 1.0 / math.sqrt(HEAD_SIZE)
    table = page_table
    prior_keys = gathered_keys[table].reshape(per_group, page_count * page_rows, channel_count)
    prior_values = gathered_values[table].reshape(per_group, page_count * page_rows, channel_count)
    attended = paged_attention(
        queries, prior_keys, prior_values, cached_lens, group_fanout, scale_factor
    )
    load_counts, offsets_all = (
        lax.all_gather(new_counts, "req", axis=0, tiled=True),
        lax.all_gather(deal_offset, "req", axis=0, tiled=True),
    )
    totals = jnp.sum(load_counts.reshape(groups, per_group), axis=1)
    rank_ids = jnp.arange(groups, dtype=jnp.int32)
    lead_in = jnp.remainder(rank_ids[None, :] - offsets_all[:, None], groups)
    shares = jnp.maximum((totals[:, None] - lead_in + groups - 1) // groups, 0)
    starts = jnp.cumsum(shares, axis=0) - shares
    placed = deal(attended, new_counts, lead_in, shares, starts, totals, balanced)
    partial_sum = project(placed, out_weight)
    width = residual.shape[1]
    own_cols = lax.axis_index("head") * width
    own_part = lax.dynamic_slice_in_dim(partial_sum, own_cols, width, 1)
    own_part = own_part.astype(jnp.bfloat16).astype(jnp.float32) + residual.astype(jnp.float32)
    partial_sum = lax.dynamic_update_slice_in_dim(partial_sum, own_part, own_cols, 1)
    hidden = head_total(partial_sum).astype(jnp.bfloat16)
    return (hidden, gathered_keys, gathered_values)


def solution(mesh):
    placed = (
        P("req", "head"),
        P("req", "head"),
        P("req", "head"),
        P("req", None, "head"),
        P("req", None, "head"),
        P("req", None),
        P("req"),
        P("req"),
        P("req"),
        P("req", "head"),
        P("head", "req"),
    )
    return jax.shard_map(
        local,
        mesh=mesh,
        in_specs=placed,
        out_specs=(P("req", "head"), P("req", None, "head"), P("req", None, "head")),
        check_vma=False,
    )
```
